128 devices in a mesh: grp: 32 (over z, y, core), head: 4 (over x).
Axes of the slice: x: 4, y: 4, z: 4, core: 2. Of those that a mesh axis runs over, the one named last changes fastest.
Arguments:
- activations: bfloat16 [1024, 4096], P('grp', 'head'), may hold values from -1.5 to 1.5
- ln_gain: bfloat16 [4096], replicated, may hold values from 0.099609375 to 1.8984375
- ln_bias: bfloat16 [4096], replicated, may hold values from -3 to 3
- w_qkv: bfloat16 [4096, 3, 4096], P('grp', None, 'head'), may hold values from -0.09375 to 0.09375
- prefix_keys: bfloat16 [64, 1024, 4096], P('grp', None, 'head')
- prefix_values: bfloat16 [64, 1024, 4096], P('grp', None, 'head'), may hold values from -6 to 6
- own_keys: bfloat16 [1024, 32, 4096], P('grp', None, 'head'), may hold values from -6 to 6
- own_values: bfloat16 [1024, 32, 4096], P('grp', None, 'head'), may hold values from -6 to 6
- prompt_len: int32 [64], P('grp'), may hold values from 64 to 1024, as said below
- own_len: int32 [1024], P('grp'), may hold values from 1 to 32, as said below
- w_attn_out: bfloat16 [256, 16, 4096], P('grp', 'head'), may hold values from -0.09375 to 0.09375
- w_in: bfloat16 [4096, 16384], P(None, ('grp', 'head')), may hold values from -0.09375 to 0.09375
- b_in: bfloat16 [16384], P(('grp', 'head')), may hold values from -4 to 4
- w_down: bfloat16 [16384, 4096], P(('grp', 'head')), may hold values from -0.046875 to 0.046875
- b_down: bfloat16 [4096], P('head'), may hold values from -3 to 3
Outputs:
- layer_out: bfloat16 [1024, 4096], P('grp', 'head')
The draws below stay inside these ranges and needn't reach their ends.
Inputs may be any that keep to these rules, and one draw needn't show every extreme that they name: `prompt_len`: some group's prompt has exactly 1024 tokens and some has 64. `own_len`: some request has exactly 32 own tokens.
All inputs are finite; a program needn't handle non-finite values.
Results may differ from the reference program's by a relative error of at most 0.034.
Values may be sent and summed in bfloat16 or wider, within the bound.
No kernel may reach another device: no remote copies, remote signals or barrier semaphores. Data moves between devices by JAX's collectives and lax.ppermute only.
A program may use at most 128 MiB of HBM per device.

```python
import math
import jax
import jax.numpy as jnp
from jax import lax

D = 4096
HEADS = 16
HS = 256
ROT = 64
FF = 16384
GSIZE = 16
OWN = 32
PMAX = 1024
GROUPS = 64
REQS = 1024
N_GRP = 32


def draw_prompt_len(key, part):
    first, second, third = jax.random.split(key, 3)
    lowest = PMAX // 16
    spread = jax.random.randint(first, (GROUPS,), 0, 257)
    lengths = lowest + (PMAX - lowest) * spread * spread // 65536
    top = jax.random.randint(second, (), 0, GROUPS)
    bottom = (top + 1 + jax.random.randint(third, (), 0, GROUPS - 1)) % GROUPS
    places = jnp.arange(GROUPS)
    lengths = jnp.where(places == top, PMAX, lengths)
    lengths = jnp.where(places == bottom, lowest, lengths)
    return lengths.astype(jnp.int32)


def draw_own_len(key, part):
    first, second = jax.random.split(key)
    counts = jax.random.randint(first, (REQS,), 1, OWN + 1)
    top = jax.random.randint(second, (), 0, REQS)
    return jnp.where(jnp.arange(REQS) == top, OWN, counts).astype(jnp.int32)


def draw_prefix_keys(key, part):
    first = jax.random.fold_in(key, 0)
    base = jnp.clip(jax.random.normal(first, (GROUPS, PMAX, D), jnp.float32), -4.0, 4.0)
    return base.astype(jnp.bfloat16)


def level_of(key, dims, shards, least, high):
    factor_of = 1.0
    for dim, shards_of in shards:
        heights = jax.random.uniform(jax.random.fold_in(jax.random.fold_in(key, 6), dim), (shards_of,), jnp.float32, least / len(shards), high / len(shards))
        factor_of = factor_of * jnp.repeat(jnp.exp(heights), dims[dim] // shards_of).reshape((-1,) + (1,) * (len(dims) - 1 - dim))
    return factor_of


def bell_draw(stream_key, extent, scale, reach, shards=(), held_as=jnp.bfloat16):
    level = level_of(stream_key, extent, shards, -0.22, 0.18) if shards else 1.0
    result = jax.random.normal(stream_key, extent, jnp.float32) * scale * level
    return jnp.minimum(jnp.maximum(result, -reach), reach).astype(held_as)


def setup_inputs(seed: int = 0) -> dict:
    seeds = jax.random.split(jax.random.key(seed), 16)
    return {
        "activations": bell_draw(seeds[0], (REQS, D), 0.25, 1.5, ((0, 32), (1, 4))),
        "ln_gain": jnp.clip(1.0 + 0.18 * jax.random.normal(seeds[1], (D,), jnp.float32), 0.099609375, 1.8984375).astype(jnp.bfloat16),
        "ln_bias": bell_draw(seeds[2], (D,), 0.5, 3.0),
        "w_qkv": bell_draw(seeds[3], (D, 3, D), D ** -0.5, 0.09375, ((0, 32), (2, 4))),
        "prefix_keys": draw_prefix_keys(jax.random.fold_in(seeds[15], 71), 0),
        "prefix_values": bell_draw(seeds[5], (GROUPS, PMAX, D), 1.0, 6.0, ((0, 32), (2, 4))),
        "own_keys": bell_draw(seeds[6], (REQS, OWN, D), 1.0, 6.0, ((0, 32), (2, 4))),
        "own_values": bell_draw(seeds[7], (REQS, OWN, D), 1.0, 6.0, ((0, 32), (2, 4))),
        "prompt_len": draw_prompt_len(jax.random.fold_in(seeds[15], 71), 0),
        "own_len": draw_own_len(jax.random.fold_in(seeds[15], 71), 0),
        "w_attn_out": bell_draw(seeds[10], (HS, HEADS, D), D ** -0.5, 0.09375, ((0, 32), (1, 4))),
        "w_in": bell_draw(seeds[11], (D, FF), D ** -0.5, 0.09375, ((1, 128),)),
        "b_in": bell_draw(seeds[12], (FF,), 1.0, 4.0, ((0, 128),)),
        "w_down": bell_draw(seeds[13], (FF, D), FF ** -0.5, 0.046875, ((0, 128),)),
        "b_down": bell_draw(seeds[14], (D,), 0.5, 3.0, ((0, 4),)),
    }


def rounded(values):
    return lax.optimization_barrier(values.astype(jnp.bfloat16)).astype(jnp.float32)

def normalize(rows, gain, shift):
    floats = rows.astype(jnp.float32)
    center = floats - lax.optimization_barrier(jnp.mean(floats, axis=-1, keepdims=True))
    spread = lax.optimization_barrier(jnp.mean(center * center, axis=-1, keepdims=True))
    return (center * lax.rsqrt(spread + 1e-05) * gain.astype(jnp.float32) + shift.astype(jnp.float32)).astype(jnp.bfloat16)

def rotate(values, positions):
    half = ROT // 2
    index = jnp.arange(half, dtype=jnp.float32)
    freqs = jnp.power(jnp.float32(10000.0), -2.0 * index / ROT)
    angle = positions[:, None, None] * freqs[None, None, :]
    cosine = jnp.cos(angle)
    sine = jnp.sin(angle)
    pairs = values[..., :ROT].reshape(values.shape[:-1] + (half, 2))
    first = pairs[..., 0]
    second = pairs[..., 1]
    turned = jnp.stack([first * cosine - second * sine, second * cosine + first * sine], axis=-1)
    turned = turned.reshape(values.shape[:-1] + (ROT,))
    return jnp.concatenate([turned, values[..., ROT:]], axis=-1)

def one_group(inputs):
    query, key_new, value_new, pre_keys, pre_vals, mine_keys, mine_vals, plength, olength = inputs
    scale = 1.0 / math.sqrt(HS)
    qfloat = query.astype(jnp.float32)
    pre_keys = pre_keys.reshape(PMAX, HEADS, HS).astype(jnp.float32)
    pre_vals = pre_vals.reshape(PMAX, HEADS, HS).astype(jnp.float32)
    mine_keys = mine_keys.astype(jnp.float32)
    mine_vals = mine_vals.astype(jnp.float32)
    pre_scores = jnp.einsum('qhd,jhd->qhj', qfloat, pre_keys) * scale
    pre_scores = jnp.where(jnp.arange(PMAX)[None, None, :] < plength, pre_scores, -jnp.inf)
    own_scores = jnp.einsum('qhd,qthd->qht', qfloat, mine_keys) * scale
    own_scores = jnp.where(jnp.arange(OWN)[None, None, :] < olength[:, None, None], own_scores, -jnp.inf)
    self_scores = lax.optimization_barrier(jnp.sum(qfloat * key_new.astype(jnp.float32), axis=-1)) * scale
    peak = jnp.maximum(jnp.maximum(lax.optimization_barrier(jnp.max(pre_scores, axis=-1)), lax.optimization_barrier(jnp.max(own_scores, axis=-1))), self_scores)
    pre_exp = jnp.exp(pre_scores - peak[..., None])
    own_exp = jnp.exp(own_scores - peak[..., None])
    self_exp = jnp.exp(self_scores - peak)
    denom = lax.optimization_barrier(jnp.sum(pre_exp, axis=-1)) + lax.optimization_barrier(jnp.sum(own_exp, axis=-1)) + self_exp
    mixed = jnp.einsum('qhj,jhd->qhd', rounded(pre_exp), pre_vals)
    mixed = mixed + jnp.einsum('qht,qthd->qhd', rounded(own_exp), mine_vals)
    mixed = mixed + rounded(self_exp)[..., None] * value_new.astype(jnp.float32)
    return (mixed / denom[..., None]).astype(jnp.bfloat16)

def reference(activations, ln_gain, ln_bias, w_qkv, prefix_keys, prefix_values, own_keys, own_values, prompt_len, own_len, w_attn_out, w_in, b_in, w_down, b_down):
    normed = normalize(activations, ln_gain, ln_bias)
    width = D // N_GRP

    def add_block(running, block):
        rows = lax.dynamic_slice_in_dim(normed, block * width, width, 1)
        weights = lax.dynamic_slice_in_dim(w_qkv, block * width, width, 0)
        term = jnp.einsum('rf,fch->rch', rows.astype(jnp.float32), weights.astype(jnp.float32))
        return (running + rounded(term), None)
    qkv, unused = lax.scan(add_block, jnp.zeros((REQS, 3, D), jnp.float32), jnp.arange(N_GRP, dtype=jnp.int32))
    member = jnp.arange(REQS, dtype=jnp.int32) // GSIZE
    positions = (prompt_len[member] + own_len).astype(jnp.float32)
    query = rotate(qkv[:, 0].reshape(REQS, HEADS, HS), positions).astype(jnp.bfloat16)
    key_new = rotate(qkv[:, 1].reshape(REQS, HEADS, HS), positions).astype(jnp.bfloat16)
    value_new = qkv[:, 2].reshape(REQS, HEADS, HS).astype(jnp.bfloat16)
    attended = lax.map(one_group, (query.reshape(GROUPS, GSIZE, HEADS, HS), key_new.reshape(GROUPS, GSIZE, HEADS, HS), value_new.reshape(GROUPS, GSIZE, HEADS, HS), prefix_keys, prefix_values, own_keys.reshape(GROUPS, GSIZE, OWN, HEADS, HS), own_values.reshape(GROUPS, GSIZE, OWN, HEADS, HS), prompt_len, own_len.reshape(GROUPS, GSIZE)))
    attended = attended.reshape(REQS, HEADS, HS)
    hidden = jax.nn.gelu(jnp.dot(normed, w_in, preferred_element_type=jnp.float32) + b_in.astype(jnp.float32), approximate=True).astype(jnp.bfloat16)
    attn_sum = jnp.einsum('rkd,dko->ro', attended.astype(jnp.float32), w_attn_out.astype(jnp.float32))
    mlp_sum = jnp.dot(hidden, w_down, preferred_element_type=jnp.float32)
    total = activations.astype(jnp.float32) + b_down.astype(jnp.float32) + attn_sum + mlp_sum
    return total.astype(jnp.bfloat16)
```

```python
import math

import jax
import jax.numpy as jnp
from jax import lax
from jax.sharding import PartitionSpec as P

HS = 256
ROT = 64
GSIZE = 16


def normalize(rows, gain, shift):
    floats = rows.astype(jnp.float32)
    center = floats - jnp.mean(floats, axis=-1, keepdims=True)
    spread = jnp.mean(center * center, axis=-1, keepdims=True)
    return (
        center * lax.rsqrt(spread + 1e-05) * gain.astype(jnp.float32) + shift.astype(jnp.float32)
    ).astype(jnp.bfloat16)


def rotate(values, positions):
    half = ROT // 2
    index = jnp.arange(half, dtype=jnp.float32)
    freqs = jnp.power(jnp.float32(10000.0), -2.0 * index / ROT)
    angle = positions[:, None, None] * freqs[None, None, :]
    cosine = jnp.cos(angle)
    sine = jnp.sin(angle)
    pairs = values[..., :ROT].reshape(values.shape[:-1] + (half, 2))
    first = pairs[..., 0]
    second = pairs[..., 1]
    turned = jnp.stack([first * cosine - second * sine, second * cosine + first * sine], axis=-1)
    turned = turned.reshape(values.shape[:-1] + (ROT,))
    return jnp.concatenate([turned, values[..., ROT:]], axis=-1)


def local(
    activations,
    ln_gain,
    ln_bias,
    w_qkv,
    prefix_keys,
    prefix_values,
    own_keys,
    own_values,
    prompt_len,
    own_len,
    w_attn_out,
    w_in,
    b_in,
    w_down,
    b_down,
):
    grp_count = lax.axis_size("grp")
    head_count = lax.axis_size("head")
    width_here = activations.shape[1]
    full_rows = lax.all_gather(activations, "head", axis=1, tiled=True)
    normed = normalize(full_rows, ln_gain, ln_bias)
    local_rows = normed.shape[0]
    groups_here = prompt_len.shape[0]
    columns = lax.all_to_all(normed, "grp", split_axis=1, concat_axis=0, tiled=True)
    qkv = lax.psum_scatter(
        jnp.einsum("rf,fch->rch", columns, w_qkv, preferred_element_type=jnp.float32).astype(
            jnp.bfloat16
        ),
        "grp",
        scatter_dimension=0,
        tiled=True,
    ).astype(jnp.float32)
    heads_here = w_qkv.shape[2] // HS
    member = (jnp.arange(local_rows) // GSIZE)[:, None] == jnp.arange(groups_here)[None, :]
    row_prompt = jnp.sum(jnp.where(member, prompt_len[None, :], 0), axis=1)
    positions = (row_prompt + own_len).astype(jnp.float32)
    query = rotate(qkv[:, 0].reshape(local_rows, heads_here, HS), positions).astype(jnp.bfloat16)
    key_new = rotate(qkv[:, 1].reshape(local_rows, heads_here, HS), positions).astype(jnp.bfloat16)
    value_new = qkv[:, 2].reshape(local_rows, heads_here, HS).astype(jnp.bfloat16)
    scale = 1.0 / math.sqrt(HS)
    longest = prefix_keys.shape[1]
    own_count = own_keys.shape[1]
    grouped = query.reshape(groups_here, GSIZE, heads_here, HS)
    pre_keys = prefix_keys.reshape(groups_here, longest, heads_here, HS)
    pre_vals = prefix_values.reshape(groups_here, longest, heads_here, HS)
    mine_keys = own_keys.reshape(local_rows, own_count, heads_here, HS)
    mine_vals = own_values.reshape(local_rows, own_count, heads_here, HS)
    pre_scores = (
        jnp.einsum("gqhd,gjhd->gqhj", grouped, pre_keys, preferred_element_type=jnp.float32) * scale
    )
    pre_scores = jnp.where(
        jnp.arange(longest)[None, None, None, :] < prompt_len[:, None, None, None],
        pre_scores,
        -jnp.inf,
    )
    own_scores = (
        jnp.einsum("rhd,rthd->rht", query, mine_keys, preferred_element_type=jnp.float32) * scale
    )
    own_scores = jnp.where(
        jnp.arange(own_count)[None, None, :] < own_len[:, None, None], own_scores, -jnp.inf
    )
    self_scores = (
        jnp.einsum("rhd,rhd->rh", query, key_new, preferred_element_type=jnp.float32) * scale
    )
    pre_peak = jnp.max(pre_scores, axis=-1).reshape(local_rows, heads_here)
    peak = jnp.maximum(jnp.maximum(pre_peak, jnp.max(own_scores, axis=-1)), self_scores)
    pre_exp = jnp.exp(pre_scores - peak.reshape(groups_here, GSIZE, heads_here)[..., None])
    own_exp = jnp.exp(own_scores - peak[..., None])
    self_exp = jnp.exp(self_scores - peak)
    denom = (
        jnp.sum(pre_exp, axis=-1).reshape(local_rows, heads_here)
        + jnp.sum(own_exp, axis=-1)
        + self_exp
    )
    mixed = jnp.einsum(
        "gqhj,gjhd->gqhd",
        pre_exp.astype(jnp.bfloat16),
        pre_vals,
        preferred_element_type=jnp.float32,
    )
    mixed = mixed.reshape(local_rows, heads_here, HS)
    mixed = mixed + jnp.einsum(
        "rht,rthd->rhd", own_exp.astype(jnp.bfloat16), mine_vals, preferred_element_type=jnp.float32
    )
    mixed = mixed + self_exp.astype(jnp.bfloat16).astype(jnp.float32)[..., None] * value_new.astype(
        jnp.float32
    )
    attended = (mixed / denom[..., None]).astype(jnp.bfloat16)
    transposed = jnp.transpose(attended, (2, 1, 0))
    slices = lax.all_to_all(transposed, "grp", split_axis=0, concat_axis=2, tiled=True)
    dim_here = slices.shape[0]
    hidden = jax.nn.gelu(
        jnp.dot(
            lax.all_gather(normed, "grp", axis=0, tiled=True),
            w_in,
            preferred_element_type=jnp.float32,
        )
        + b_in.astype(jnp.float32),
        approximate=True,
    ).astype(jnp.bfloat16)
    units = hidden.shape[1]
    mlp_part = jnp.einsum(
        "gri,ihf->ghrf",
        hidden.reshape(grp_count, local_rows, units),
        w_down.reshape(units, head_count, width_here),
        preferred_element_type=jnp.float32,
    )
    attn_part = jnp.einsum(
        "dkgr,dkhf->ghrf",
        slices.reshape(dim_here, heads_here, grp_count, local_rows),
        w_attn_out.reshape(dim_here, heads_here, head_count, width_here),
        preferred_element_type=jnp.float32,
    )
    combined = (mlp_part + attn_part).reshape(grp_count * head_count * local_rows, width_here)
    pieces = lax.all_to_all(
        combined.astype(jnp.bfloat16).reshape(grp_count * head_count, local_rows, width_here),
        ("grp", "head"),
        0,
        0,
        tiled=True,
    )
    summed = jnp.sum(pieces.astype(jnp.float32), axis=0)
    total = activations.astype(jnp.float32) + b_down.astype(jnp.float32)[None, :] + summed
    return total.astype(jnp.bfloat16)


def solution(mesh):
    in_specs = (
        P("grp", "head"),
        P(),
        P(),
        P("grp", None, "head"),
        P("grp", None, "head"),
        P("grp", None, "head"),
        P("grp", None, "head"),
        P("grp", None, "head"),
        P("grp"),
        P("grp"),
        P("grp", "head", None),
        P(None, ("grp", "head")),
        P(("grp", "head")),
        P(("grp", "head"), None),
        P("head"),
    )
    out_specs = P("grp", "head")
    return jax.shard_map(local, mesh=mesh, in_specs=in_specs, out_specs=out_specs, check_vma=False)
```

```python
import math

import jax
import jax.numpy as jnp
from jax import lax
from jax.sharding import PartitionSpec as P

HS = 256
ROT = 64
GSIZE = 16


def normalize(rows, gain, shift):
    floats = rows.astype(jnp.float32)
    center = floats - jnp.mean(floats, axis=-1, keepdims=True)
    spread = jnp.mean(center * center, axis=-1, keepdims=True)
    return (
        center * lax.rsqrt(spread + 1e-05) * gain.astype(jnp.float32) + shift.astype(jnp.float32)
    ).astype(jnp.bfloat16)


def rotate(values, positions):
    half = ROT // 2
    index = jnp.arange(half, dtype=jnp.float32)
    freqs = jnp.power(jnp.float32(10000.0), -2.0 * index / ROT)
    angle = positions[:, None, None] * freqs[None, None, :]
    cosine = jnp.cos(angle)
    sine = jnp.sin(angle)
    pairs = values[..., :ROT].reshape(values.shape[:-1] + (half, 2))
    first = pairs[..., 0]
    second = pairs[..., 1]
    turned = jnp.stack([first * cosine - second * sine, second * cosine + first * sine], axis=-1)
    turned = turned.reshape(values.shape[:-1] + (ROT,))
    return jnp.concatenate([turned, values[..., ROT:]], axis=-1)


def local(
    activations,
    ln_gain,
    ln_bias,
    w_qkv,
    prefix_keys,
    prefix_values,
    own_keys,
    own_values,
    prompt_len,
    own_len,
    w_attn_out,
    w_in,
    b_in,
    w_down,
    b_down,
):
    grp_count = lax.axis_size("grp")
    head_count = lax.axis_size("head")
    width_here = activations.shape[1]
    full_rows = lax.all_gather(activations, "head", axis=1, tiled=True)
    normed = normalize(full_rows, ln_gain, ln_bias)
    local_rows = normed.shape[0]
    groups_here = prompt_len.shape[0]
    columns = lax.all_to_all(normed, "grp", split_axis=1, concat_axis=0, tiled=True)
    qkv = lax.psum_scatter(
        jnp.einsum("rf,fch->rch", columns, w_qkv, preferred_element_type=jnp.float32).astype(
            jnp.bfloat16
        ),
        "grp",
        scatter_dimension=0,
        tiled=True,
    ).astype(jnp.float32)
    heads_here = w_qkv.shape[2] // HS
    member = (jnp.arange(local_rows) // GSIZE)[:, None] == jnp.arange(groups_here)[None, :]
    row_prompt = jnp.sum(jnp.where(member, prompt_len[None, :], 0), axis=1)
    positions = (row_prompt + own_len).astype(jnp.float32)
    query = rotate(qkv[:, 0].reshape(local_rows, heads_here, HS), positions).astype(jnp.bfloat16)
    key_new = rotate(qkv[:, 1].reshape(local_rows, heads_here, HS), positions).astype(jnp.bfloat16)
    value_new = qkv[:, 2].reshape(local_rows, heads_here, HS).astype(jnp.bfloat16)
    scale = 1.0 / math.sqrt(HS)
    longest = prefix_keys.shape[1]
    own_count = own_keys.shape[1]
    grouped = query.reshape(groups_here, GSIZE, heads_here, HS)
    pre_keys = prefix_keys.reshape(groups_here, longest, heads_here, HS)
    pre_vals = prefix_values.reshape(groups_here, longest, heads_here, HS)
    mine_keys = own_keys.reshape(local_rows, own_count, heads_here, HS)
    mine_vals = own_values.reshape(local_rows, own_count, heads_here, HS)
    pre_scores = (
        jnp.einsum("gqhd,gjhd->gqhj", grouped, pre_keys, preferred_element_type=jnp.float32) * scale
    )
    pre_scores = jnp.where(
        jnp.arange(longest)[None, None, None, :] < prompt_len[:, None, None, None],
        pre_scores,
        -jnp.inf,
    )
    own_scores = (
        jnp.einsum("rhd,rthd->rht", query, mine_keys, preferred_element_type=jnp.float32) * scale
    )
    own_scores = jnp.where(
        jnp.arange(own_count)[None, None, :] < own_len[:, None, None], own_scores, -jnp.inf
    )
    self_scores = (
        jnp.einsum("rhd,rhd->rh", query, key_new, preferred_element_type=jnp.float32) * scale
    )
    pre_peak = jnp.max(pre_scores, axis=-1).reshape(local_rows, heads_here)
    peak = jnp.maximum(jnp.maximum(pre_peak, jnp.max(own_scores, axis=-1)), self_scores)
    pre_exp = jnp.exp(pre_scores - peak.reshape(groups_here, GSIZE, heads_here)[..., None])
    own_exp = jnp.exp(own_scores - peak[..., None])
    self_exp = jnp.exp(self_scores - peak)
    denom = (
        jnp.sum(pre_exp, axis=-1).reshape(local_rows, heads_here)
        + jnp.sum(own_exp, axis=-1)
        + self_exp
    )
    mixed = jnp.einsum(
        "gqhj,gjhd->gqhd",
        pre_exp.astype(jnp.bfloat16),
        pre_vals,
        preferred_element_type=jnp.float32,
    )
    mixed = mixed.reshape(local_rows, heads_here, HS)
    mixed = mixed + jnp.einsum(
        "rht,rthd->rhd", own_exp.astype(jnp.bfloat16), mine_vals, preferred_element_type=jnp.float32
    )
    mixed = mixed + self_exp.astype(jnp.bfloat16).astype(jnp.float32)[..., None] * value_new.astype(
        jnp.float32
    )
    attended = (mixed / denom[..., None]).astype(jnp.bfloat16)
    transposed = jnp.transpose(attended, (2, 1, 0))
    slices = lax.all_to_all(transposed, "grp", split_axis=0, concat_axis=2, tiled=True)
    slices = lax.all_gather(slices, "head", axis=1, tiled=True)
    dim_here = slices.shape[0]
    out_blocks = lax.all_to_all(
        w_attn_out.reshape(dim_here, heads_here, head_count, width_here),
        "head",
        split_axis=2,
        concat_axis=1,
        tiled=True,
    ).reshape(dim_here, heads_here * head_count, width_here)
    units = w_in.shape[1]
    down_blocks = lax.all_to_all(
        w_down.reshape(units, head_count, width_here), "head", split_axis=1, concat_axis=0, tiled=True
    ).reshape(units * head_count, width_here)
    hidden = jax.nn.gelu(
        jnp.dot(
            lax.all_gather(normed, "grp", axis=0, tiled=True),
            w_in,
            preferred_element_type=jnp.float32,
        )
        + b_in.astype(jnp.float32),
        approximate=True,
    ).astype(jnp.bfloat16)
    hidden = lax.all_gather(hidden, "head", axis=1, tiled=True)
    mlp_part = jnp.dot(hidden, down_blocks, preferred_element_type=jnp.float32)
    attn_part = jnp.einsum("dkr,dkf->rf", slices, out_blocks, preferred_element_type=jnp.float32)
    combined = mlp_part + attn_part
    pieces = lax.all_to_all(
        combined.astype(jnp.bfloat16).reshape(grp_count, local_rows, width_here),
        "grp",
        0,
        0,
        tiled=True,
    )
    summed = jnp.sum(pieces.astype(jnp.float32), axis=0)
    total = activations.astype(jnp.float32) + b_down.astype(jnp.float32)[None, :] + summed
    return total.astype(jnp.bfloat16)


def solution(mesh):
    in_specs = (
        P("grp", "head"),
        P(),
        P(),
        P("grp", None, "head"),
        P("grp", None, "head"),
        P("grp", None, "head"),
        P("grp", None, "head"),
        P("grp", None, "head"),
        P("grp"),
        P("grp"),
        P("grp", "head", None),
        P(None, ("grp", "head")),
        P(("grp", "head")),
        P(("grp", "head"), None),
        P("head"),
    )
    out_specs = P("grp", "head")
    return jax.shard_map(local, mesh=mesh, in_specs=in_specs, out_specs=out_specs, check_vma=False)
```

```python
import math

import jax
import jax.numpy as jnp
from jax import lax
from jax.sharding import PartitionSpec as P

HS = 256
ROT = 64
GSIZE = 16


def normalize(rows, gain, shift):
    floats = rows.astype(jnp.float32)
    center = floats - jnp.mean(floats, axis=-1, keepdims=True)
    spread = jnp.mean(center * center, axis=-1, keepdims=True)
    return (
        center * lax.rsqrt(spread + 1e-05) * gain.astype(jnp.float32) + shift.astype(jnp.float32)
    ).astype(jnp.bfloat16)


def rotate(values, positions):
    half = ROT // 2
    index = jnp.arange(half, dtype=jnp.float32)
    freqs = jnp.power(jnp.float32(10000.0), -2.0 * index / ROT)
    angle = positions[:, None, None] * freqs[None, None, :]
    cosine = jnp.cos(angle)
    sine = jnp.sin(angle)
    pairs = values[..., :ROT].reshape(values.shape[:-1] + (half, 2))
    first = pairs[..., 0]
    second = pairs[..., 1]
    turned = jnp.stack([first * cosine - second * sine, second * cosine + first * sine], axis=-1)
    turned = turned.reshape(values.shape[:-1] + (ROT,))
    return jnp.concatenate([turned, values[..., ROT:]], axis=-1)


def local(
    activations,
    ln_gain,
    ln_bias,
    w_qkv,
    prefix_keys,
    prefix_values,
    own_keys,
    own_values,
    prompt_len,
    own_len,
    w_attn_out,
    w_in,
    b_in,
    w_down,
    b_down,
):
    grp_count = lax.axis_size("grp")
    head_count = lax.axis_size("head")
    width_here = activations.shape[1]
    full_rows = lax.all_gather(activations, "head", axis=1, tiled=True)
    normed = normalize(full_rows, ln_gain, ln_bias)
    local_rows = normed.shape[0]
    groups_here = prompt_len.shape[0]
    gathered = lax.all_gather(normed, "grp", axis=0, tiled=True)
    block = w_qkv.shape[0]
    columns = lax.dynamic_slice_in_dim(gathered, lax.axis_index("grp") * block, block, axis=1)
    qkv = lax.psum_scatter(
        jnp.einsum("rf,fch->rch", columns, w_qkv, preferred_element_type=jnp.float32).astype(
            jnp.bfloat16
        ),
        "grp",
        scatter_dimension=0,
        tiled=True,
    ).astype(jnp.float32)
    heads_here = w_qkv.shape[2] // HS
    member = (jnp.arange(local_rows) // GSIZE)[:, None] == jnp.arange(groups_here)[None, :]
    row_prompt = jnp.sum(jnp.where(member, prompt_len[None, :], 0), axis=1)
    positions = (row_prompt + own_len).astype(jnp.float32)
    query = rotate(qkv[:, 0].reshape(local_rows, heads_here, HS), positions).astype(jnp.bfloat16)
    key_new = rotate(qkv[:, 1].reshape(local_rows, heads_here, HS), positions).astype(jnp.bfloat16)
    value_new = qkv[:, 2].reshape(local_rows, heads_here, HS).astype(jnp.bfloat16)
    scale = 1.0 / math.sqrt(HS)
    longest = prefix_keys.shape[1]
    own_count = own_keys.shape[1]
    grouped = query.reshape(groups_here, GSIZE, heads_here, HS)
    pre_keys = prefix_keys.reshape(groups_here, longest, heads_here, HS)
    pre_vals = prefix_values.reshape(groups_here, longest, heads_here, HS)
    mine_keys = own_keys.reshape(local_rows, own_count, heads_here, HS)
    mine_vals = own_values.reshape(local_rows, own_count, heads_here, HS)
    pre_scores = (
        jnp.einsum("gqhd,gjhd->gqhj", grouped, pre_keys, preferred_element_type=jnp.float32) * scale
    )
    pre_scores = jnp.where(
        jnp.arange(longest)[None, None, None, :] < prompt_len[:, None, None, None],
        pre_scores,
        -jnp.inf,
    )
    own_scores = (
        jnp.einsum("rhd,rthd->rht", query, mine_keys, preferred_element_type=jnp.float32) * scale
    )
    own_scores = jnp.where(
        jnp.arange(own_count)[None, None, :] < own_len[:, None, None], own_scores, -jnp.inf
    )
    self_scores = (
        jnp.einsum("rhd,rhd->rh", query, key_new, preferred_element_type=jnp.float32) * scale
    )
    pre_peak = jnp.max(pre_scores, axis=-1).reshape(local_rows, heads_here)
    peak = jnp.maximum(jnp.maximum(pre_peak, jnp.max(own_scores, axis=-1)), self_scores)
    pre_exp = jnp.exp(pre_scores - peak.reshape(groups_here, GSIZE, heads_here)[..., None])
    own_exp = jnp.exp(own_scores - peak[..., None])
    self_exp = jnp.exp(self_scores - peak)
    denom = (
        jnp.sum(pre_exp, axis=-1).reshape(local_rows, heads_here)
        + jnp.sum(own_exp, axis=-1)
        + self_exp
    )
    mixed = jnp.einsum(
        "gqhj,gjhd->gqhd",
        pre_exp.astype(jnp.bfloat16),
        pre_vals,
        preferred_element_type=jnp.float32,
    )
    mixed = mixed.reshape(local_rows, heads_here, HS)
    mixed = mixed + jnp.einsum(
        "rht,rthd->rhd", own_exp.astype(jnp.bfloat16), mine_vals, preferred_element_type=jnp.float32
    )
    mixed = mixed + self_exp.astype(jnp.bfloat16).astype(jnp.float32)[..., None] * value_new.astype(
        jnp.float32
    )
    attended = (mixed / denom[..., None]).astype(jnp.bfloat16)
    transposed = jnp.transpose(attended, (2, 1, 0))
    slices = lax.all_to_all(transposed, "grp", split_axis=0, concat_axis=2, tiled=True)
    slices = lax.all_gather(slices, "head", axis=1, tiled=True)
    dim_here = slices.shape[0]
    out_blocks = lax.all_to_all(
        w_attn_out.reshape(dim_here, heads_here, head_count, width_here),
        "head",
        split_axis=2,
        concat_axis=1,
        tiled=True,
    ).reshape(dim_here, heads_here * head_count, width_here)
    units = w_in.shape[1]
    down_blocks = lax.all_to_all(
        w_down.reshape(units, head_count, width_here), "head", split_axis=1, concat_axis=0, tiled=True
    ).reshape(units * head_count, width_here)
    hidden = jax.nn.gelu(
        jnp.dot(
            gathered,
            w_in,
            preferred_element_type=jnp.float32,
        )
        + b_in.astype(jnp.float32),
        approximate=True,
    ).astype(jnp.bfloat16)
    hidden = lax.all_gather(hidden, "head", axis=1, tiled=True)
    mlp_part = jnp.dot(hidden, down_blocks, preferred_element_type=jnp.float32)
    attn_part = jnp.einsum("dkr,dkf->rf", slices, out_blocks, preferred_element_type=jnp.float32)
    combined = mlp_part + attn_part
    pieces = lax.all_to_all(
        combined.astype(jnp.bfloat16).reshape(grp_count, local_rows, width_here),
        "grp",
        0,
        0,
        tiled=True,
    )
    summed = jnp.sum(pieces.astype(jnp.float32), axis=0)
    total = activations.astype(jnp.float32) + b_down.astype(jnp.float32)[None, :] + summed
    return total.astype(jnp.bfloat16)


def solution(mesh):
    in_specs = (
        P("grp", "head"),
        P(),
        P(),
        P("grp", None, "head"),
        P("grp", None, "head"),
        P("grp", None, "head"),
        P("grp", None, "head"),
        P("grp", None, "head"),
        P("grp"),
        P("grp"),
        P("grp", "head", None),
        P(None, ("grp", "head")),
        P(("grp", "head")),
        P(("grp", "head"), None),
        P("head"),
    )
    out_specs = P("grp", "head")
    return jax.shard_map(local, mesh=mesh, in_specs=in_specs, out_specs=out_specs, check_vma=False)
```

```python
import math

import jax
import jax.numpy as jnp
from jax import lax
from jax.sharding import PartitionSpec as P

HS = 256
ROT = 64
GSIZE = 16


def normalize(rows, gain, shift):
    floats = rows.astype(jnp.float32)
    center = floats - jnp.mean(floats, axis=-1, keepdims=True)
    spread = jnp.mean(center * center, axis=-1, keepdims=True)
    return (
        center * lax.rsqrt(spread + 1e-05) * gain.astype(jnp.float32) + shift.astype(jnp.float32)
    ).astype(jnp.bfloat16)


def rotate(values, positions):
    half = ROT // 2
    index = jnp.arange(half, dtype=jnp.float32)
    freqs = jnp.power(jnp.float32(10000.0), -2.0 * index / ROT)
    angle = positions[:, None, None] * freqs[None, None, :]
    cosine = jnp.cos(angle)
    sine = jnp.sin(angle)
    pairs = values[..., :ROT].reshape(values.shape[:-1] + (half, 2))
    first = pairs[..., 0]
    second = pairs[..., 1]
    turned = jnp.stack([first * cosine - second * sine, second * cosine + first * sine], axis=-1)
    turned = turned.reshape(values.shape[:-1] + (ROT,))
    return jnp.concatenate([turned, values[..., ROT:]], axis=-1)


def local(
    activations,
    ln_gain,
    ln_bias,
    w_qkv,
    prefix_keys,
    prefix_values,
    own_keys,
    own_values,
    prompt_len,
    own_len,
    w_attn_out,
    w_in,
    b_in,
    w_down,
    b_down,
):
    grp_count = lax.axis_size("grp")
    head_count = lax.axis_size("head")
    width_here = activations.shape[1]
    full_rows = lax.all_gather(activations, "head", axis=1, tiled=True)
    normed = normalize(full_rows, ln_gain, ln_bias)
    local_rows = normed.shape[0]
    groups_here = prompt_len.shape[0]
    gathered = lax.all_gather(normed, "grp", axis=0, tiled=True)
    block = w_qkv.shape[0]
    pair_rows = normed.reshape(local_rows, grp_count // 2, 2 * block)
    columns = lax.all_to_all(
        jnp.repeat(pair_rows, 2, axis=1), "grp", split_axis=1, concat_axis=0, tiled=True
    ).reshape(grp_count * local_rows, 2 * block)
    parity = lax.axis_index("grp") % 2
    half = w_qkv.shape[2] // 2
    own = lax.dynamic_slice_in_dim(w_qkv, parity * half, half, axis=2)
    other = lax.dynamic_slice_in_dim(w_qkv, (1 - parity) * half, half, axis=2)
    sibling = lax.ppermute(other, "grp", [(i, i ^ 1) for i in range(grp_count)])
    pair_weights = jnp.where(
        parity == 0,
        jnp.concatenate([own, sibling], axis=0),
        jnp.concatenate([sibling, own], axis=0),
    )
    term = jnp.einsum(
        "rf,fch->rch", columns, pair_weights, preferred_element_type=jnp.float32
    ).astype(jnp.bfloat16)
    received = lax.all_to_all(
        term.reshape(grp_count, local_rows, 3, half), "grp", 0, 0, tiled=True
    ).reshape(grp_count // 2, 2, local_rows, 3, half)
    qkv = jnp.sum(received.astype(jnp.float32), axis=0)
    qkv = jnp.transpose(qkv, (1, 2, 0, 3)).reshape(local_rows, 3, 2 * half)
    heads_here = w_qkv.shape[2] // HS
    member = (jnp.arange(local_rows) // GSIZE)[:, None] == jnp.arange(groups_here)[None, :]
    row_prompt = jnp.sum(jnp.where(member, prompt_len[None, :], 0), axis=1)
    positions = (row_prompt + own_len).astype(jnp.float32)
    query = rotate(qkv[:, 0].reshape(local_rows, heads_here, HS), positions).astype(jnp.bfloat16)
    key_new = rotate(qkv[:, 1].reshape(local_rows, heads_here, HS), positions).astype(jnp.bfloat16)
    value_new = qkv[:, 2].reshape(local_rows, heads_here, HS).astype(jnp.bfloat16)
    scale = 1.0 / math.sqrt(HS)
    longest = prefix_keys.shape[1]
    own_count = own_keys.shape[1]
    grouped = query.reshape(groups_here, GSIZE, heads_here, HS)
    pre_keys = prefix_keys.reshape(groups_here, longest, heads_here, HS)
    pre_vals = prefix_values.reshape(groups_here, longest, heads_here, HS)
    mine_keys = own_keys.reshape(local_rows, own_count, heads_here, HS)
    mine_vals = own_values.reshape(local_rows, own_count, heads_here, HS)
    pre_scores = (
        jnp.einsum("gqhd,gjhd->gqhj", grouped, pre_keys, preferred_element_type=jnp.float32) * scale
    )
    pre_scores = jnp.where(
        jnp.arange(longest)[None, None, None, :] < prompt_len[:, None, None, None],
        pre_scores,
        -jnp.inf,
    )
    own_scores = (
        jnp.einsum("rhd,rthd->rht", query, mine_keys, preferred_element_type=jnp.float32) * scale
    )
    own_scores = jnp.where(
        jnp.arange(own_count)[None, None, :] < own_len[:, None, None], own_scores, -jnp.inf
    )
    self_scores = (
        jnp.einsum("rhd,rhd->rh", query, key_new, preferred_element_type=jnp.float32) * scale
    )
    pre_peak = jnp.max(pre_scores, axis=-1).reshape(local_rows, heads_here)
    peak = jnp.maximum(jnp.maximum(pre_peak, jnp.max(own_scores, axis=-1)), self_scores)
    pre_exp = jnp.exp(pre_scores - peak.reshape(groups_here, GSIZE, heads_here)[..., None])
    own_exp = jnp.exp(own_scores - peak[..., None])
    self_exp = jnp.exp(self_scores - peak)
    denom = (
        jnp.sum(pre_exp, axis=-1).reshape(local_rows, heads_here)
        + jnp.sum(own_exp, axis=-1)
        + self_exp
    )
    mixed = jnp.einsum(
        "gqhj,gjhd->gqhd",
        pre_exp.astype(jnp.bfloat16),
        pre_vals,
        preferred_element_type=jnp.float32,
    )
    mixed = mixed.reshape(local_rows, heads_here, HS)
    mixed = mixed + jnp.einsum(
        "rht,rthd->rhd", own_exp.astype(jnp.bfloat16), mine_vals, preferred_element_type=jnp.float32
    )
    mixed = mixed + self_exp.astype(jnp.bfloat16).astype(jnp.float32)[..., None] * value_new.astype(
        jnp.float32
    )
    attended = (mixed / denom[..., None]).astype(jnp.bfloat16)
    transposed = jnp.transpose(attended, (2, 1, 0))
    slices = lax.all_to_all(transposed, "grp", split_axis=0, concat_axis=2, tiled=True)
    slices = lax.all_gather(slices, "head", axis=1, tiled=True)
    dim_here = slices.shape[0]
    out_blocks = lax.all_to_all(
        w_attn_out.reshape(dim_here, heads_here, head_count, width_here),
        "head",
        split_axis=2,
        concat_axis=1,
        tiled=True,
    ).reshape(dim_here, heads_here * head_count, width_here)
    units = w_in.shape[1]
    down_blocks = lax.all_to_all(
        w_down.reshape(units, head_count, width_here), "head", split_axis=1, concat_axis=0, tiled=True
    ).reshape(units * head_count, width_here)
    hidden = jax.nn.gelu(
        jnp.dot(
            gathered,
            w_in,
            preferred_element_type=jnp.float32,
        )
        + b_in.astype(jnp.float32),
        approximate=True,
    ).astype(jnp.bfloat16)
    hidden = lax.all_gather(hidden, "head", axis=1, tiled=True)
    mlp_part = jnp.dot(hidden, down_blocks, preferred_element_type=jnp.float32)
    attn_part = jnp.einsum("dkr,dkf->rf", slices, out_blocks, preferred_element_type=jnp.float32)
    combined = mlp_part + attn_part
    pieces = lax.all_to_all(
        combined.astype(jnp.bfloat16).reshape(grp_count, local_rows, width_here),
        "grp",
        0,
        0,
        tiled=True,
    )
    summed = jnp.sum(pieces.astype(jnp.float32), axis=0)
    total = activations.astype(jnp.float32) + b_down.astype(jnp.float32)[None, :] + summed
    return total.astype(jnp.bfloat16)


def solution(mesh):
    in_specs = (
        P("grp", "head"),
        P(),
        P(),
        P("grp", None, "head"),
        P("grp", None, "head"),
        P("grp", None, "head"),
        P("grp", None, "head"),
        P("grp", None, "head"),
        P("grp"),
        P("grp"),
        P("grp", "head", None),
        P(None, ("grp", "head")),
        P(("grp", "head")),
        P(("grp", "head"), None),
        P("head"),
    )
    out_specs = P("grp", "head")
    return jax.shard_map(local, mesh=mesh, in_specs=in_specs, out_specs=out_specs, check_vma=False)
```

```python
import math

import jax
import jax.numpy as jnp
from jax import lax
from jax.sharding import PartitionSpec as P

HS = 256
ROT = 64
GSIZE = 16


def normalize(rows, gain, shift):
    floats = rows.astype(jnp.float32)
    center = floats - jnp.mean(floats, axis=-1, keepdims=True)
    spread = jnp.mean(center * center, axis=-1, keepdims=True)
    return (
        center * lax.rsqrt(spread + 1e-05) * gain.astype(jnp.float32) + shift.astype(jnp.float32)
    ).astype(jnp.bfloat16)


def rotate(values, positions):
    half = ROT // 2
    index = jnp.arange(half, dtype=jnp.float32)
    freqs = jnp.power(jnp.float32(10000.0), -2.0 * index / ROT)
    angle = positions[:, None, None] * freqs[None, None, :]
    cosine = jnp.cos(angle)
    sine = jnp.sin(angle)
    pairs = values[..., :ROT].reshape(values.shape[:-1] + (half, 2))
    first = pairs[..., 0]
    second = pairs[..., 1]
    turned = jnp.stack([first * cosine - second * sine, second * cosine + first * sine], axis=-1)
    turned = turned.reshape(values.shape[:-1] + (ROT,))
    return jnp.concatenate([turned, values[..., ROT:]], axis=-1)


def head_exchange(pieces, axis):
    count = lax.axis_size("head")
    here = lax.axis_index("head")
    received = []
    for shift in range(count):
        piece = lax.dynamic_index_in_dim(pieces, (here + shift) % count, axis, keepdims=False)
        if shift:
            piece = lax.ppermute(piece, "head", [(i, (i + shift) % count) for i in range(count)])
        received.append(piece)
    stacked = jnp.stack(received, axis=0)
    return jnp.take(stacked, (here - jnp.arange(count)) % count, axis=0)


def head_gather(piece):
    count = lax.axis_size("head")
    here = lax.axis_index("head")
    received = [piece]
    for shift in range(1, count):
        received.append(lax.ppermute(piece, "head", [(i, (i + shift) % count) for i in range(count)]))
    stacked = jnp.stack(received, axis=0)
    return jnp.take(stacked, (here - jnp.arange(count)) % count, axis=0)


def local(
    activations,
    ln_gain,
    ln_bias,
    w_qkv,
    prefix_keys,
    prefix_values,
    own_keys,
    own_values,
    prompt_len,
    own_len,
    w_attn_out,
    w_in,
    b_in,
    w_down,
    b_down,
):
    grp_count = lax.axis_size("grp")
    head_count = lax.axis_size("head")
    width_here = activations.shape[1]
    full_rows = jnp.moveaxis(head_gather(activations), 0, 1).reshape(activations.shape[0], -1)
    normed = normalize(full_rows, ln_gain, ln_bias)
    local_rows = normed.shape[0]
    groups_here = prompt_len.shape[0]
    gathered = lax.all_gather(normed, "grp", axis=0, tiled=True)
    block = w_qkv.shape[0]
    pair_rows = normed.reshape(local_rows, grp_count // 2, 2 * block)
    columns = lax.all_to_all(
        jnp.repeat(pair_rows, 2, axis=1), "grp", split_axis=1, concat_axis=0, tiled=True
    ).reshape(grp_count * local_rows, 2 * block)
    parity = lax.axis_index("grp") % 2
    half = w_qkv.shape[2] // 2
    own = lax.dynamic_slice_in_dim(w_qkv, parity * half, half, axis=2)
    other = lax.dynamic_slice_in_dim(w_qkv, (1 - parity) * half, half, axis=2)
    sibling = lax.ppermute(other, "grp", [(i, i ^ 1) for i in range(grp_count)])
    pair_weights = jnp.where(
        parity == 0,
        jnp.concatenate([own, sibling], axis=0),
        jnp.concatenate([sibling, own], axis=0),
    )
    term = jnp.einsum(
        "rf,fch->rch", columns, pair_weights, preferred_element_type=jnp.float32
    ).astype(jnp.bfloat16)
    received = lax.all_to_all(
        term.reshape(grp_count, local_rows, 3, half), "grp", 0, 0, tiled=True
    ).reshape(grp_count // 2, 2, local_rows, 3, half)
    qkv = jnp.sum(received.astype(jnp.float32), axis=0)
    qkv = jnp.transpose(qkv, (1, 2, 0, 3)).reshape(local_rows, 3, 2 * half)
    heads_here = w_qkv.shape[2] // HS
    member = (jnp.arange(local_rows) // GSIZE)[:, None] == jnp.arange(groups_here)[None, :]
    row_prompt = jnp.sum(jnp.where(member, prompt_len[None, :], 0), axis=1)
    positions = (row_prompt + own_len).astype(jnp.float32)
    query = rotate(qkv[:, 0].reshape(local_rows, heads_here, HS), positions).astype(jnp.bfloat16)
    key_new = rotate(qkv[:, 1].reshape(local_rows, heads_here, HS), positions).astype(jnp.bfloat16)
    value_new = qkv[:, 2].reshape(local_rows, heads_here, HS).astype(jnp.bfloat16)
    scale = 1.0 / math.sqrt(HS)
    longest = prefix_keys.shape[1]
    own_count = own_keys.shape[1]
    grouped = query.reshape(groups_here, GSIZE, heads_here, HS)
    pre_keys = prefix_keys.reshape(groups_here, longest, heads_here, HS)
    pre_vals = prefix_values.reshape(groups_here, longest, heads_here, HS)
    mine_keys = own_keys.reshape(local_rows, own_count, heads_here, HS)
    mine_vals = own_values.reshape(local_rows, own_count, heads_here, HS)
    pre_scores = (
        jnp.einsum("gqhd,gjhd->gqhj", grouped, pre_keys, preferred_element_type=jnp.float32) * scale
    )
    pre_scores = jnp.where(
        jnp.arange(longest)[None, None, None, :] < prompt_len[:, None, None, None],
        pre_scores,
        -jnp.inf,
    )
    own_scores = (
        jnp.einsum("rhd,rthd->rht", query, mine_keys, preferred_element_type=jnp.float32) * scale
    )
    own_scores = jnp.where(
        jnp.arange(own_count)[None, None, :] < own_len[:, None, None], own_scores, -jnp.inf
    )
    self_scores = (
        jnp.einsum("rhd,rhd->rh", query, key_new, preferred_element_type=jnp.float32) * scale
    )
    pre_peak = jnp.max(pre_scores, axis=-1).reshape(local_rows, heads_here)
    peak = jnp.maximum(jnp.maximum(pre_peak, jnp.max(own_scores, axis=-1)), self_scores)
    pre_exp = jnp.exp(pre_scores - peak.reshape(groups_here, GSIZE, heads_here)[..., None])
    own_exp = jnp.exp(own_scores - peak[..., None])
    self_exp = jnp.exp(self_scores - peak)
    denom = (
        jnp.sum(pre_exp, axis=-1).reshape(local_rows, heads_here)
        + jnp.sum(own_exp, axis=-1)
        + self_exp
    )
    mixed = jnp.einsum(
        "gqhj,gjhd->gqhd",
        pre_exp.astype(jnp.bfloat16),
        pre_vals,
        preferred_element_type=jnp.float32,
    )
    mixed = mixed.reshape(local_rows, heads_here, HS)
    mixed = mixed + jnp.einsum(
        "rht,rthd->rhd", own_exp.astype(jnp.bfloat16), mine_vals, preferred_element_type=jnp.float32
    )
    mixed = mixed + self_exp.astype(jnp.bfloat16).astype(jnp.float32)[..., None] * value_new.astype(
        jnp.float32
    )
    attended = (mixed / denom[..., None]).astype(jnp.bfloat16)
    transposed = jnp.transpose(attended, (2, 1, 0))
    slices = lax.all_to_all(transposed, "grp", split_axis=0, concat_axis=2, tiled=True)
    dim_here = slices.shape[0]
    slices = jnp.moveaxis(head_gather(slices), 0, 1).reshape(dim_here, heads_here * head_count, -1)
    out_blocks = head_exchange(
        w_attn_out.reshape(dim_here, heads_here, head_count, width_here), 2
    )
    out_blocks = jnp.moveaxis(out_blocks, 0, 1).reshape(dim_here, heads_here * head_count, width_here)
    units = w_in.shape[1]
    down_blocks = head_exchange(w_down.reshape(units, head_count, width_here), 1).reshape(
        units * head_count, width_here
    )
    hidden = jax.nn.gelu(
        jnp.dot(
            gathered,
            w_in,
            preferred_element_type=jnp.float32,
        )
        + b_in.astype(jnp.float32),
        approximate=True,
    ).astype(jnp.bfloat16)
    hidden = lax.all_gather(hidden, "head", axis=1, tiled=True)
    mlp_part = jnp.dot(hidden, down_blocks, preferred_element_type=jnp.float32)
    attn_part = jnp.einsum("dkr,dkf->rf", slices, out_blocks, preferred_element_type=jnp.float32)
    combined = mlp_part + attn_part
    pieces = lax.all_to_all(
        combined.astype(jnp.bfloat16).reshape(grp_count, local_rows, width_here),
        "grp",
        0,
        0,
        tiled=True,
    )
    summed = jnp.sum(pieces.astype(jnp.float32), axis=0)
    total = activations.astype(jnp.float32) + b_down.astype(jnp.float32)[None, :] + summed
    return total.astype(jnp.bfloat16)


def solution(mesh):
    in_specs = (
        P("grp", "head"),
        P(),
        P(),
        P("grp", None, "head"),
        P("grp", None, "head"),
        P("grp", None, "head"),
        P("grp", None, "head"),
        P("grp", None, "head"),
        P("grp"),
        P("grp"),
        P("grp", "head", None),
        P(None, ("grp", "head")),
        P(("grp", "head")),
        P(("grp", "head"), None),
        P("head"),
    )
    out_specs = P("grp", "head")
    return jax.shard_map(local, mesh=mesh, in_specs=in_specs, out_specs=out_specs, check_vma=False)
```

```python
import math

import jax
import jax.numpy as jnp
from jax import lax
from jax.sharding import PartitionSpec as P

HS = 256
ROT = 64
GSIZE = 16


def normalize(rows, gain, shift):
    floats = rows.astype(jnp.float32)
    center = floats - jnp.mean(floats, axis=-1, keepdims=True)
    spread = jnp.mean(center * center, axis=-1, keepdims=True)
    return (
        center * lax.rsqrt(spread + 1e-05) * gain.astype(jnp.float32) + shift.astype(jnp.float32)
    ).astype(jnp.bfloat16)


def rotate(values, positions):
    half = ROT // 2
    index = jnp.arange(half, dtype=jnp.float32)
    freqs = jnp.power(jnp.float32(10000.0), -2.0 * index / ROT)
    angle = positions[:, None, None] * freqs[None, None, :]
    cosine = jnp.cos(angle)
    sine = jnp.sin(angle)
    pairs = values[..., :ROT].reshape(values.shape[:-1] + (half, 2))
    first = pairs[..., 0]
    second = pairs[..., 1]
    turned = jnp.stack([first * cosine - second * sine, second * cosine + first * sine], axis=-1)
    turned = turned.reshape(values.shape[:-1] + (ROT,))
    return jnp.concatenate([turned, values[..., ROT:]], axis=-1)


def head_exchange(pieces, axis):
    count = lax.axis_size("head")
    here = lax.axis_index("head")
    received = []
    for shift in range(count):
        piece = lax.dynamic_index_in_dim(pieces, (here + shift) % count, axis, keepdims=False)
        if shift:
            piece = lax.ppermute(piece, "head", [(i, (i + shift) % count) for i in range(count)])
        received.append(piece)
    stacked = jnp.stack(received, axis=0)
    return jnp.take(stacked, (here - jnp.arange(count)) % count, axis=0)


def head_gather(piece):
    count = lax.axis_size("head")
    here = lax.axis_index("head")
    received = [piece]
    for shift in range(1, count):
        received.append(lax.ppermute(piece, "head", [(i, (i + shift) % count) for i in range(count)]))
    stacked = jnp.stack(received, axis=0)
    return jnp.take(stacked, (here - jnp.arange(count)) % count, axis=0)


def local(
    activations,
    ln_gain,
    ln_bias,
    w_qkv,
    prefix_keys,
    prefix_values,
    own_keys,
    own_values,
    prompt_len,
    own_len,
    w_attn_out,
    w_in,
    b_in,
    w_down,
    b_down,
):
    grp_count = lax.axis_size("grp")
    head_count = lax.axis_size("head")
    width_here = activations.shape[1]
    full_rows = jnp.moveaxis(head_gather(activations), 0, 1).reshape(activations.shape[0], -1)
    normed = normalize(full_rows, ln_gain, ln_bias)
    local_rows = normed.shape[0]
    groups_here = prompt_len.shape[0]
    gathered = lax.all_gather(normed, "grp", axis=0, tiled=True)
    block = w_qkv.shape[0]
    pair_rows = normed.reshape(local_rows, grp_count // 2, 2 * block)
    columns = lax.all_to_all(
        jnp.repeat(pair_rows, 2, axis=1), "grp", split_axis=1, concat_axis=0, tiled=True
    ).reshape(grp_count * local_rows, 2 * block)
    parity = lax.axis_index("grp") % 2
    half = w_qkv.shape[2] // 2
    own = lax.dynamic_slice_in_dim(w_qkv, parity * half, half, axis=2)
    other = lax.dynamic_slice_in_dim(w_qkv, (1 - parity) * half, half, axis=2)
    sibling = lax.ppermute(other, "grp", [(i, i ^ 1) for i in range(grp_count)])
    pair_weights = jnp.where(
        parity == 0,
        jnp.concatenate([own, sibling], axis=0),
        jnp.concatenate([sibling, own], axis=0),
    )
    term = jnp.einsum(
        "rf,fch->rch", columns, pair_weights, preferred_element_type=jnp.float32
    ).astype(jnp.bfloat16)
    received = lax.all_to_all(
        term.reshape(grp_count, local_rows, 3, half), "grp", 0, 0, tiled=True
    ).reshape(grp_count // 2, 2, local_rows, 3, half)
    qkv = jnp.sum(received.astype(jnp.float32), axis=0)
    qkv = jnp.transpose(qkv, (1, 2, 0, 3)).reshape(local_rows, 3, 2 * half)
    heads_here = w_qkv.shape[2] // HS
    member = (jnp.arange(local_rows) // GSIZE)[:, None] == jnp.arange(groups_here)[None, :]
    row_prompt = jnp.sum(jnp.where(member, prompt_len[None, :], 0), axis=1)
    positions = (row_prompt + own_len).astype(jnp.float32)
    query = rotate(qkv[:, 0].reshape(local_rows, heads_here, HS), positions).astype(jnp.bfloat16)
    key_new = rotate(qkv[:, 1].reshape(local_rows, heads_here, HS), positions).astype(jnp.bfloat16)
    value_new = qkv[:, 2].reshape(local_rows, heads_here, HS).astype(jnp.bfloat16)
    scale = 1.0 / math.sqrt(HS)
    longest = prefix_keys.shape[1]
    own_count = own_keys.shape[1]
    grouped = query.reshape(groups_here, GSIZE, heads_here, HS)
    pre_keys = prefix_keys.reshape(groups_here, longest, heads_here, HS)
    pre_vals = prefix_values.reshape(groups_here, longest, heads_here, HS)
    mine_keys = own_keys.reshape(local_rows, own_count, heads_here, HS)
    mine_vals = own_values.reshape(local_rows, own_count, heads_here, HS)
    pre_scores = (
        jnp.einsum("gqhd,gjhd->gqhj", grouped, pre_keys, preferred_element_type=jnp.float32) * scale
    )
    pre_scores = jnp.where(
        jnp.arange(longest)[None, None, None, :] < prompt_len[:, None, None, None],
        pre_scores,
        -jnp.inf,
    )
    own_scores = (
        jnp.einsum("rhd,rthd->rht", query, mine_keys, preferred_element_type=jnp.float32) * scale
    )
    own_scores = jnp.where(
        jnp.arange(own_count)[None, None, :] < own_len[:, None, None], own_scores, -jnp.inf
    )
    self_scores = (
        jnp.einsum("rhd,rhd->rh", query, key_new, preferred_element_type=jnp.float32) * scale
    )
    pre_peak = jnp.max(pre_scores, axis=-1).reshape(local_rows, heads_here)
    peak = jnp.maximum(jnp.maximum(pre_peak, jnp.max(own_scores, axis=-1)), self_scores)
    pre_exp = jnp.exp(pre_scores - peak.reshape(groups_here, GSIZE, heads_here)[..., None])
    own_exp = jnp.exp(own_scores - peak[..., None])
    self_exp = jnp.exp(self_scores - peak)
    denom = (
        jnp.sum(pre_exp, axis=-1).reshape(local_rows, heads_here)
        + jnp.sum(own_exp, axis=-1)
        + self_exp
    )
    mixed = jnp.einsum(
        "gqhj,gjhd->gqhd",
        pre_exp.astype(jnp.bfloat16),
        pre_vals,
        preferred_element_type=jnp.float32,
    )
    mixed = mixed.reshape(local_rows, heads_here, HS)
    mixed = mixed + jnp.einsum(
        "rht,rthd->rhd", own_exp.astype(jnp.bfloat16), mine_vals, preferred_element_type=jnp.float32
    )
    mixed = mixed + self_exp.astype(jnp.bfloat16).astype(jnp.float32)[..., None] * value_new.astype(
        jnp.float32
    )
    attended = (mixed / denom[..., None]).astype(jnp.bfloat16)
    transposed = jnp.transpose(attended, (2, 1, 0))
    slices = lax.all_to_all(transposed, "grp", split_axis=0, concat_axis=2, tiled=True)
    dim_here = slices.shape[0]
    slices = jnp.moveaxis(head_gather(slices), 0, 1).reshape(dim_here, heads_here * head_count, -1)
    out_blocks = head_exchange(
        w_attn_out.reshape(dim_here, heads_here, head_count, width_here), 2
    )
    out_blocks = jnp.moveaxis(out_blocks, 0, 1).reshape(dim_here, heads_here * head_count, width_here)
    units = w_in.shape[1]
    down_blocks = head_exchange(w_down.reshape(units, head_count, width_here), 1).reshape(
        units * head_count, width_here
    )
    hidden = jax.nn.gelu(
        jnp.dot(
            gathered,
            w_in,
            preferred_element_type=jnp.float32,
        )
        + b_in.astype(jnp.float32),
        approximate=True,
    ).astype(jnp.bfloat16)
    hidden = lax.all_gather(hidden, "head", axis=1, tiled=True)
    mlp_part = jnp.dot(hidden, down_blocks, preferred_element_type=jnp.float32)
    attn_part = jnp.einsum("dkr,dkf->rf", slices, out_blocks, preferred_element_type=jnp.float32)
    combined = mlp_part + attn_part
    half_width = width_here // 2
    mine = lax.dynamic_slice_in_dim(combined, parity * half_width, half_width, axis=1)
    theirs = lax.dynamic_slice_in_dim(combined, (1 - parity) * half_width, half_width, axis=1)
    got = lax.ppermute(
        theirs.astype(jnp.bfloat16), "grp", [(i, i ^ 1) for i in range(grp_count)]
    )
    pair_sum = (mine + got.astype(jnp.float32)).astype(jnp.bfloat16)
    pieces = lax.all_to_all(
        pair_sum.reshape(grp_count, local_rows, half_width), "grp", 0, 0, tiled=True
    ).reshape(grp_count // 2, 2, local_rows, half_width)
    summed = jnp.sum(pieces.astype(jnp.float32), axis=0)
    summed = jnp.transpose(summed, (1, 0, 2)).reshape(local_rows, width_here)
    total = activations.astype(jnp.float32) + b_down.astype(jnp.float32)[None, :] + summed
    return total.astype(jnp.bfloat16)


def solution(mesh):
    in_specs = (
        P("grp", "head"),
        P(),
        P(),
        P("grp", None, "head"),
        P("grp", None, "head"),
        P("grp", None, "head"),
        P("grp", None, "head"),
        P("grp", None, "head"),
        P("grp"),
        P("grp"),
        P("grp", "head", None),
        P(None, ("grp", "head")),
        P(("grp", "head")),
        P(("grp", "head"), None),
        P("head"),
    )
    out_specs = P("grp", "head")
    return jax.shard_map(local, mesh=mesh, in_specs=in_specs, out_specs=out_specs, check_vma=False)
```

```python
import math

import jax
import jax.numpy as jnp
from jax import lax
from jax.sharding import PartitionSpec as P

HS = 256
ROT = 64
GSIZE = 16


def normalize(rows, gain, shift):
    floats = rows.astype(jnp.float32)
    center = floats - jnp.mean(floats, axis=-1, keepdims=True)
    spread = jnp.mean(center * center, axis=-1, keepdims=True)
    return (
        center * lax.rsqrt(spread + 1e-05) * gain.astype(jnp.float32) + shift.astype(jnp.float32)
    ).astype(jnp.bfloat16)


def rotate(values, positions):
    half = ROT // 2
    index = jnp.arange(half, dtype=jnp.float32)
    freqs = jnp.power(jnp.float32(10000.0), -2.0 * index / ROT)
    angle = positions[:, None, None] * freqs[None, None, :]
    cosine = jnp.cos(angle)
    sine = jnp.sin(angle)
    pairs = values[..., :ROT].reshape(values.shape[:-1] + (half, 2))
    first = pairs[..., 0]
    second = pairs[..., 1]
    turned = jnp.stack([first * cosine - second * sine, second * cosine + first * sine], axis=-1)
    turned = turned.reshape(values.shape[:-1] + (ROT,))
    return jnp.concatenate([turned, values[..., ROT:]], axis=-1)


def head_exchange(pieces, axis):
    count = lax.axis_size("head")
    here = lax.axis_index("head")
    received = []
    for shift in range(count):
        piece = lax.dynamic_index_in_dim(pieces, (here + shift) % count, axis, keepdims=False)
        if shift:
            piece = lax.ppermute(piece, "head", [(i, (i + shift) % count) for i in range(count)])
        received.append(piece)
    stacked = jnp.stack(received, axis=0)
    return jnp.take(stacked, (here - jnp.arange(count)) % count, axis=0)


def head_gather(piece):
    count = lax.axis_size("head")
    here = lax.axis_index("head")
    received = [piece]
    for shift in range(1, count):
        received.append(lax.ppermute(piece, "head", [(i, (i + shift) % count) for i in range(count)]))
    stacked = jnp.stack(received, axis=0)
    return jnp.take(stacked, (here - jnp.arange(count)) % count, axis=0)


def local(
    activations,
    ln_gain,
    ln_bias,
    w_qkv,
    prefix_keys,
    prefix_values,
    own_keys,
    own_values,
    prompt_len,
    own_len,
    w_attn_out,
    w_in,
    b_in,
    w_down,
    b_down,
):
    grp_count = lax.axis_size("grp")
    head_count = lax.axis_size("head")
    width_here = activations.shape[1]
    full_rows = jnp.moveaxis(head_gather(activations), 0, 1).reshape(activations.shape[0], -1)
    normed = normalize(full_rows, ln_gain, ln_bias)
    local_rows = normed.shape[0]
    groups_here = prompt_len.shape[0]
    quarter = lax.dynamic_slice_in_dim(normed, lax.axis_index("head") * width_here, width_here, axis=1)
    gathered = lax.all_gather(quarter, "grp", axis=0, tiled=True)
    block = w_qkv.shape[0]
    pair_rows = normed.reshape(local_rows, grp_count // 2, 2 * block)
    columns = lax.all_to_all(
        jnp.repeat(pair_rows, 2, axis=1), "grp", split_axis=1, concat_axis=0, tiled=True
    ).reshape(grp_count * local_rows, 2 * block)
    parity = lax.axis_index("grp") % 2
    half = w_qkv.shape[2] // 2
    own = lax.dynamic_slice_in_dim(w_qkv, parity * half, half, axis=2)
    other = lax.dynamic_slice_in_dim(w_qkv, (1 - parity) * half, half, axis=2)
    sibling = lax.ppermute(other, "grp", [(i, i ^ 1) for i in range(grp_count)])
    pair_weights = jnp.where(
        parity == 0,
        jnp.concatenate([own, sibling], axis=0),
        jnp.concatenate([sibling, own], axis=0),
    )
    term = jnp.einsum(
        "rf,fch->rch", columns, pair_weights, preferred_element_type=jnp.float32
    ).astype(jnp.bfloat16)
    received = lax.all_to_all(
        term.reshape(grp_count, local_rows, 3, half), "grp", 0, 0, tiled=True
    ).reshape(grp_count // 2, 2, local_rows, 3, half)
    qkv = jnp.sum(received.astype(jnp.float32), axis=0)
    qkv = jnp.transpose(qkv, (1, 2, 0, 3)).reshape(local_rows, 3, 2 * half)
    heads_here = w_qkv.shape[2] // HS
    member = (jnp.arange(local_rows) // GSIZE)[:, None] == jnp.arange(groups_here)[None, :]
    row_prompt = jnp.sum(jnp.where(member, prompt_len[None, :], 0), axis=1)
    positions = (row_prompt + own_len).astype(jnp.float32)
    query = rotate(qkv[:, 0].reshape(local_rows, heads_here, HS), positions).astype(jnp.bfloat16)
    key_new = rotate(qkv[:, 1].reshape(local_rows, heads_here, HS), positions).astype(jnp.bfloat16)
    value_new = qkv[:, 2].reshape(local_rows, heads_here, HS).astype(jnp.bfloat16)
    scale = 1.0 / math.sqrt(HS)
    longest = prefix_keys.shape[1]
    own_count = own_keys.shape[1]
    grouped = query.reshape(groups_here, GSIZE, heads_here, HS)
    pre_keys = prefix_keys.reshape(groups_here, longest, heads_here, HS)
    pre_vals = prefix_values.reshape(groups_here, longest, heads_here, HS)
    mine_keys = own_keys.reshape(local_rows, own_count, heads_here, HS)
    mine_vals = own_values.reshape(local_rows, own_count, heads_here, HS)
    pre_scores = (
        jnp.einsum("gqhd,gjhd->gqhj", grouped, pre_keys, preferred_element_type=jnp.float32) * scale
    )
    pre_scores = jnp.where(
        jnp.arange(longest)[None, None, None, :] < prompt_len[:, None, None, None],
        pre_scores,
        -jnp.inf,
    )
    own_scores = (
        jnp.einsum("rhd,rthd->rht", query, mine_keys, preferred_element_type=jnp.float32) * scale
    )
    own_scores = jnp.where(
        jnp.arange(own_count)[None, None, :] < own_len[:, None, None], own_scores, -jnp.inf
    )
    self_scores = (
        jnp.einsum("rhd,rhd->rh", query, key_new, preferred_element_type=jnp.float32) * scale
    )
    pre_peak = jnp.max(pre_scores, axis=-1).reshape(local_rows, heads_here)
    peak = jnp.maximum(jnp.maximum(pre_peak, jnp.max(own_scores, axis=-1)), self_scores)
    pre_exp = jnp.exp(pre_scores - peak.reshape(groups_here, GSIZE, heads_here)[..., None])
    own_exp = jnp.exp(own_scores - peak[..., None])
    self_exp = jnp.exp(self_scores - peak)
    denom = (
        jnp.sum(pre_exp, axis=-1).reshape(local_rows, heads_here)
        + jnp.sum(own_exp, axis=-1)
        + self_exp
    )
    mixed = jnp.einsum(
        "gqhj,gjhd->gqhd",
        pre_exp.astype(jnp.bfloat16),
        pre_vals,
        preferred_element_type=jnp.float32,
    )
    mixed = mixed.reshape(local_rows, heads_here, HS)
    mixed = mixed + jnp.einsum(
        "rht,rthd->rhd", own_exp.astype(jnp.bfloat16), mine_vals, preferred_element_type=jnp.float32
    )
    mixed = mixed + self_exp.astype(jnp.bfloat16).astype(jnp.float32)[..., None] * value_new.astype(
        jnp.float32
    )
    attended = (mixed / denom[..., None]).astype(jnp.bfloat16)
    transposed = jnp.transpose(attended, (2, 1, 0))
    slices = lax.all_to_all(transposed, "grp", split_axis=0, concat_axis=2, tiled=True)
    dim_here = slices.shape[0]
    slices = jnp.moveaxis(head_gather(slices), 0, 1).reshape(dim_here, heads_here * head_count, -1)
    out_blocks = head_exchange(
        w_attn_out.reshape(dim_here, heads_here, head_count, width_here), 2
    )
    out_blocks = jnp.moveaxis(out_blocks, 0, 1).reshape(dim_here, heads_here * head_count, width_here)
    units = w_in.shape[1]
    down_blocks = head_exchange(w_down.reshape(units, head_count, width_here), 1).reshape(
        units * head_count, width_here
    )
    in_blocks = head_exchange(w_in.reshape(head_count, width_here, units), 0)
    in_blocks = jnp.moveaxis(in_blocks, 0, 1).reshape(width_here, head_count * units)
    partial = jnp.dot(gathered, in_blocks, preferred_element_type=jnp.float32)
    partial = head_exchange(partial.astype(jnp.bfloat16).reshape(-1, head_count, units), 1)
    hidden = jax.nn.gelu(
        jnp.sum(partial.astype(jnp.float32), axis=0) + b_in.astype(jnp.float32),
        approximate=True,
    ).astype(jnp.bfloat16)
    hidden = lax.all_gather(hidden, "head", axis=1, tiled=True)
    mlp_part = jnp.dot(hidden, down_blocks, preferred_element_type=jnp.float32)
    attn_part = jnp.einsum("dkr,dkf->rf", slices, out_blocks, preferred_element_type=jnp.float32)
    combined = mlp_part + attn_part
    half_width = width_here // 2
    mine = lax.dynamic_slice_in_dim(combined, parity * half_width, half_width, axis=1)
    theirs = lax.dynamic_slice_in_dim(combined, (1 - parity) * half_width, half_width, axis=1)
    got = lax.ppermute(
        theirs.astype(jnp.bfloat16), "grp", [(i, i ^ 1) for i in range(grp_count)]
    )
    pair_sum = (mine + got.astype(jnp.float32)).astype(jnp.bfloat16)
    pieces = lax.all_to_all(
        pair_sum.reshape(grp_count, local_rows, half_width), "grp", 0, 0, tiled=True
    ).reshape(grp_count // 2, 2, local_rows, half_width)
    summed = jnp.sum(pieces.astype(jnp.float32), axis=0)
    summed = jnp.transpose(summed, (1, 0, 2)).reshape(local_rows, width_here)
    total = activations.astype(jnp.float32) + b_down.astype(jnp.float32)[None, :] + summed
    return total.astype(jnp.bfloat16)


def solution(mesh):
    in_specs = (
        P("grp", "head"),
        P(),
        P(),
        P("grp", None, "head"),
        P("grp", None, "head"),
        P("grp", None, "head"),
        P("grp", None, "head"),
        P("grp", None, "head"),
        P("grp"),
        P("grp"),
        P("grp", "head", None),
        P(None, ("grp", "head")),
        P(("grp", "head")),
        P(("grp", "head"), None),
        P("head"),
    )
    out_specs = P("grp", "head")
    return jax.shard_map(local, mesh=mesh, in_specs=in_specs, out_specs=out_specs, check_vma=False)
```

```python
import math

import jax
import jax.numpy as jnp
from jax import lax
from jax.sharding import PartitionSpec as P

HS = 256
ROT = 64
GSIZE = 16


def normalize(rows, gain, shift):
    floats = rows.astype(jnp.float32)
    center = floats - jnp.mean(floats, axis=-1, keepdims=True)
    spread = jnp.mean(center * center, axis=-1, keepdims=True)
    return (
        center * lax.rsqrt(spread + 1e-05) * gain.astype(jnp.float32) + shift.astype(jnp.float32)
    ).astype(jnp.bfloat16)


def rotate(values, positions):
    half = ROT // 2
    index = jnp.arange(half, dtype=jnp.float32)
    freqs = jnp.power(jnp.float32(10000.0), -2.0 * index / ROT)
    angle = positions[:, None, None] * freqs[None, None, :]
    cosine = jnp.cos(angle)
    sine = jnp.sin(angle)
    pairs = values[..., :ROT].reshape(values.shape[:-1] + (half, 2))
    first = pairs[..., 0]
    second = pairs[..., 1]
    turned = jnp.stack([first * cosine - second * sine, second * cosine + first * sine], axis=-1)
    turned = turned.reshape(values.shape[:-1] + (ROT,))
    return jnp.concatenate([turned, values[..., ROT:]], axis=-1)


def head_exchange(pieces, axis):
    count = lax.axis_size("head")
    here = lax.axis_index("head")
    received = []
    for shift in range(count):
        piece = lax.dynamic_index_in_dim(pieces, (here + shift) % count, axis, keepdims=False)
        if shift:
            piece = lax.ppermute(piece, "head", [(i, (i + shift) % count) for i in range(count)])
        received.append(piece)
    stacked = jnp.stack(received, axis=0)
    return jnp.take(stacked, (here - jnp.arange(count)) % count, axis=0)


def head_gather(piece):
    count = lax.axis_size("head")
    here = lax.axis_index("head")
    received = [piece]
    for shift in range(1, count):
        received.append(lax.ppermute(piece, "head", [(i, (i + shift) % count) for i in range(count)]))
    stacked = jnp.stack(received, axis=0)
    return jnp.take(stacked, (here - jnp.arange(count)) % count, axis=0)


def local(
    activations,
    ln_gain,
    ln_bias,
    w_qkv,
    prefix_keys,
    prefix_values,
    own_keys,
    own_values,
    prompt_len,
    own_len,
    w_attn_out,
    w_in,
    b_in,
    w_down,
    b_down,
):
    grp_count = lax.axis_size("grp")
    head_count = lax.axis_size("head")
    width_here = activations.shape[1]
    full_rows = jnp.moveaxis(head_gather(activations), 0, 1).reshape(activations.shape[0], -1)
    normed = normalize(full_rows, ln_gain, ln_bias)
    local_rows = normed.shape[0]
    groups_here = prompt_len.shape[0]
    floats = full_rows.astype(jnp.float32)
    mean = jnp.mean(floats, axis=-1, keepdims=True)
    center = floats - mean
    scale_of_row = lax.rsqrt(jnp.mean(center * center, axis=-1, keepdims=True) + 1e-05)
    row_stats = lax.all_gather(
        jnp.concatenate([mean, scale_of_row], axis=1), "grp", axis=0, tiled=True
    )
    raw_quarter = lax.all_gather(activations, "grp", axis=0, tiled=True).astype(jnp.float32)
    feature_start = lax.axis_index("head") * width_here
    gain_quarter = lax.dynamic_slice_in_dim(ln_gain, feature_start, width_here).astype(jnp.float32)
    bias_quarter = lax.dynamic_slice_in_dim(ln_bias, feature_start, width_here).astype(jnp.float32)
    gathered = (
        (raw_quarter - row_stats[:, :1]) * row_stats[:, 1:] * gain_quarter + bias_quarter
    ).astype(jnp.bfloat16)
    block = w_qkv.shape[0]
    pair_rows = normed.reshape(local_rows, grp_count // 2, 2 * block)
    columns = lax.all_to_all(
        jnp.repeat(pair_rows, 2, axis=1), "grp", split_axis=1, concat_axis=0, tiled=True
    ).reshape(grp_count * local_rows, 2 * block)
    parity = lax.axis_index("grp") % 2
    half = w_qkv.shape[2] // 2
    own = lax.dynamic_slice_in_dim(w_qkv, parity * half, half, axis=2)
    other = lax.dynamic_slice_in_dim(w_qkv, (1 - parity) * half, half, axis=2)
    sibling = lax.ppermute(other, "grp", [(i, i ^ 1) for i in range(grp_count)])
    pair_weights = jnp.where(
        parity == 0,
        jnp.concatenate([own, sibling], axis=0),
        jnp.concatenate([sibling, own], axis=0),
    )
    term = jnp.einsum(
        "rf,fch->rch", columns, pair_weights, preferred_element_type=jnp.float32
    ).astype(jnp.bfloat16)
    received = lax.all_to_all(
        term.reshape(grp_count, local_rows, 3, half), "grp", 0, 0, tiled=True
    ).reshape(grp_count // 2, 2, local_rows, 3, half)
    qkv = jnp.sum(received.astype(jnp.float32), axis=0)
    qkv = jnp.transpose(qkv, (1, 2, 0, 3)).reshape(local_rows, 3, 2 * half)
    heads_here = w_qkv.shape[2] // HS
    member = (jnp.arange(local_rows) // GSIZE)[:, None] == jnp.arange(groups_here)[None, :]
    row_prompt = jnp.sum(jnp.where(member, prompt_len[None, :], 0), axis=1)
    positions = (row_prompt + own_len).astype(jnp.float32)
    query = rotate(qkv[:, 0].reshape(local_rows, heads_here, HS), positions).astype(jnp.bfloat16)
    key_new = rotate(qkv[:, 1].reshape(local_rows, heads_here, HS), positions).astype(jnp.bfloat16)
    value_new = qkv[:, 2].reshape(local_rows, heads_here, HS).astype(jnp.bfloat16)
    scale = 1.0 / math.sqrt(HS)
    longest = prefix_keys.shape[1]
    own_count = own_keys.shape[1]
    grouped = query.reshape(groups_here, GSIZE, heads_here, HS)
    pre_keys = prefix_keys.reshape(groups_here, longest, heads_here, HS)
    pre_vals = prefix_values.reshape(groups_here, longest, heads_here, HS)
    mine_keys = own_keys.reshape(local_rows, own_count, heads_here, HS)
    mine_vals = own_values.reshape(local_rows, own_count, heads_here, HS)
    pre_scores = (
        jnp.einsum("gqhd,gjhd->gqhj", grouped, pre_keys, preferred_element_type=jnp.float32) * scale
    )
    pre_scores = jnp.where(
        jnp.arange(longest)[None, None, None, :] < prompt_len[:, None, None, None],
        pre_scores,
        -jnp.inf,
    )
    own_scores = (
        jnp.einsum("rhd,rthd->rht", query, mine_keys, preferred_element_type=jnp.float32) * scale
    )
    own_scores = jnp.where(
        jnp.arange(own_count)[None, None, :] < own_len[:, None, None], own_scores, -jnp.inf
    )
    self_scores = (
        jnp.einsum("rhd,rhd->rh", query, key_new, preferred_element_type=jnp.float32) * scale
    )
    pre_peak = jnp.max(pre_scores, axis=-1).reshape(local_rows, heads_here)
    peak = jnp.maximum(jnp.maximum(pre_peak, jnp.max(own_scores, axis=-1)), self_scores)
    pre_exp = jnp.exp(pre_scores - peak.reshape(groups_here, GSIZE, heads_here)[..., None])
    own_exp = jnp.exp(own_scores - peak[..., None])
    self_exp = jnp.exp(self_scores - peak)
    denom = (
        jnp.sum(pre_exp, axis=-1).reshape(local_rows, heads_here)
        + jnp.sum(own_exp, axis=-1)
        + self_exp
    )
    mixed = jnp.einsum(
        "gqhj,gjhd->gqhd",
        pre_exp.astype(jnp.bfloat16),
        pre_vals,
        preferred_element_type=jnp.float32,
    )
    mixed = mixed.reshape(local_rows, heads_here, HS)
    mixed = mixed + jnp.einsum(
        "rht,rthd->rhd", own_exp.astype(jnp.bfloat16), mine_vals, preferred_element_type=jnp.float32
    )
    mixed = mixed + self_exp.astype(jnp.bfloat16).astype(jnp.float32)[..., None] * value_new.astype(
        jnp.float32
    )
    attended = (mixed / denom[..., None]).astype(jnp.bfloat16)
    transposed = jnp.transpose(attended, (2, 1, 0))
    slices = lax.all_to_all(transposed, "grp", split_axis=0, concat_axis=2, tiled=True)
    dim_here = slices.shape[0]
    slices = jnp.moveaxis(head_gather(slices), 0, 1).reshape(dim_here, heads_here * head_count, -1)
    out_blocks = head_exchange(
        w_attn_out.reshape(dim_here, heads_here, head_count, width_here), 2
    )
    out_blocks = jnp.moveaxis(out_blocks, 0, 1).reshape(dim_here, heads_here * head_count, width_here)
    units = w_in.shape[1]
    down_blocks = head_exchange(w_down.reshape(units, head_count, width_here), 1).reshape(
        units * head_count, width_here
    )
    in_blocks = head_exchange(w_in.reshape(head_count, width_here, units), 0)
    in_blocks = jnp.moveaxis(in_blocks, 0, 1).reshape(width_here, head_count * units)
    partial = jnp.dot(gathered, in_blocks, preferred_element_type=jnp.float32)
    partial = head_exchange(partial.astype(jnp.bfloat16).reshape(-1, head_count, units), 1)
    hidden = jax.nn.gelu(
        jnp.sum(partial.astype(jnp.float32), axis=0) + b_in.astype(jnp.float32),
        approximate=True,
    ).astype(jnp.bfloat16)
    hidden = lax.all_gather(hidden, "head", axis=1, tiled=True)
    mlp_part = jnp.dot(hidden, down_blocks, preferred_element_type=jnp.float32)
    attn_part = jnp.einsum("dkr,dkf->rf", slices, out_blocks, preferred_element_type=jnp.float32)
    combined = mlp_part + attn_part
    half_width = width_here // 2
    mine = lax.dynamic_slice_in_dim(combined, parity * half_width, half_width, axis=1)
    theirs = lax.dynamic_slice_in_dim(combined, (1 - parity) * half_width, half_width, axis=1)
    got = lax.ppermute(
        theirs.astype(jnp.bfloat16), "grp", [(i, i ^ 1) for i in range(grp_count)]
    )
    pair_sum = (mine + got.astype(jnp.float32)).astype(jnp.bfloat16)
    pieces = lax.all_to_all(
        pair_sum.reshape(grp_count, local_rows, half_width), "grp", 0, 0, tiled=True
    ).reshape(grp_count // 2, 2, local_rows, half_width)
    summed = jnp.sum(pieces.astype(jnp.float32), axis=0)
    summed = jnp.transpose(summed, (1, 0, 2)).reshape(local_rows, width_here)
    total = activations.astype(jnp.float32) + b_down.astype(jnp.float32)[None, :] + summed
    return total.astype(jnp.bfloat16)


def solution(mesh):
    in_specs = (
        P("grp", "head"),
        P(),
        P(),
        P("grp", None, "head"),
        P("grp", None, "head"),
        P("grp", None, "head"),
        P("grp", None, "head"),
        P("grp", None, "head"),
        P("grp"),
        P("grp"),
        P("grp", "head", None),
        P(None, ("grp", "head")),
        P(("grp", "head")),
        P(("grp", "head"), None),
        P("head"),
    )
    out_specs = P("grp", "head")
    return jax.shard_map(local, mesh=mesh, in_specs=in_specs, out_specs=out_specs, check_vma=False)
```

```python
import math

import jax
import jax.numpy as jnp
from jax import lax
from jax.sharding import PartitionSpec as P

HS = 256
ROT = 64
GSIZE = 16


def normalize(rows, gain, shift):
    floats = rows.astype(jnp.float32)
    center = floats - jnp.mean(floats, axis=-1, keepdims=True)
    spread = jnp.mean(center * center, axis=-1, keepdims=True)
    return (
        center * lax.rsqrt(spread + 1e-05) * gain.astype(jnp.float32) + shift.astype(jnp.float32)
    ).astype(jnp.bfloat16)


def rotate(values, positions):
    half = ROT // 2
    index = jnp.arange(half, dtype=jnp.float32)
    freqs = jnp.power(jnp.float32(10000.0), -2.0 * index / ROT)
    angle = positions[:, None, None] * freqs[None, None, :]
    cosine = jnp.cos(angle)
    sine = jnp.sin(angle)
    pairs = values[..., :ROT].reshape(values.shape[:-1] + (half, 2))
    first = pairs[..., 0]
    second = pairs[..., 1]
    turned = jnp.stack([first * cosine - second * sine, second * cosine + first * sine], axis=-1)
    turned = turned.reshape(values.shape[:-1] + (ROT,))
    return jnp.concatenate([turned, values[..., ROT:]], axis=-1)


def head_exchange(pieces, axis):
    count = lax.axis_size("head")
    here = lax.axis_index("head")
    received = []
    for shift in range(count):
        piece = lax.dynamic_index_in_dim(pieces, (here + shift) % count, axis, keepdims=False)
        if shift:
            piece = lax.ppermute(piece, "head", [(i, (i + shift) % count) for i in range(count)])
        received.append(piece)
    stacked = jnp.stack(received, axis=0)
    return jnp.take(stacked, (here - jnp.arange(count)) % count, axis=0)


def head_gather(piece):
    count = lax.axis_size("head")
    here = lax.axis_index("head")
    received = [piece]
    for shift in range(1, count):
        received.append(lax.ppermute(piece, "head", [(i, (i + shift) % count) for i in range(count)]))
    stacked = jnp.stack(received, axis=0)
    return jnp.take(stacked, (here - jnp.arange(count)) % count, axis=0)


def local(
    activations,
    ln_gain,
    ln_bias,
    w_qkv,
    prefix_keys,
    prefix_values,
    own_keys,
    own_values,
    prompt_len,
    own_len,
    w_attn_out,
    w_in,
    b_in,
    w_down,
    b_down,
):
    grp_count = lax.axis_size("grp")
    head_count = lax.axis_size("head")
    width_here = activations.shape[1]
    full_rows = jnp.moveaxis(head_gather(activations), 0, 1).reshape(activations.shape[0], -1)
    normed = normalize(full_rows, ln_gain, ln_bias)
    local_rows = normed.shape[0]
    groups_here = prompt_len.shape[0]
    quarter = lax.dynamic_slice_in_dim(normed, lax.axis_index("head") * width_here, width_here, axis=1)
    block = w_qkv.shape[0]
    pair_rows = normed.reshape(local_rows, grp_count // 2, 2 * block)
    outgoing = jnp.concatenate(
        [
            jnp.repeat(pair_rows, 2, axis=1),
            jnp.broadcast_to(quarter[:, None, :], (local_rows, grp_count, width_here)),
        ],
        axis=2,
    )
    incoming = lax.all_to_all(outgoing, "grp", split_axis=1, concat_axis=0, tiled=True).reshape(
        grp_count * local_rows, 2 * block + width_here
    )
    columns = incoming[:, : 2 * block]
    gathered = incoming[:, 2 * block :]
    parity = lax.axis_index("grp") % 2
    half = w_qkv.shape[2] // 2
    own = lax.dynamic_slice_in_dim(w_qkv, parity * half, half, axis=2)
    other = lax.dynamic_slice_in_dim(w_qkv, (1 - parity) * half, half, axis=2)
    sibling = lax.ppermute(other, "grp", [(i, i ^ 1) for i in range(grp_count)])
    pair_weights = jnp.where(
        parity == 0,
        jnp.concatenate([own, sibling], axis=0),
        jnp.concatenate([sibling, own], axis=0),
    )
    term = jnp.einsum(
        "rf,fch->rch", columns, pair_weights, preferred_element_type=jnp.float32
    ).astype(jnp.bfloat16)
    received = lax.all_to_all(
        term.reshape(grp_count, local_rows, 3, half), "grp", 0, 0, tiled=True
    ).reshape(grp_count // 2, 2, local_rows, 3, half)
    qkv = jnp.sum(received.astype(jnp.float32), axis=0)
    qkv = jnp.transpose(qkv, (1, 2, 0, 3)).reshape(local_rows, 3, 2 * half)
    heads_here = w_qkv.shape[2] // HS
    member = (jnp.arange(local_rows) // GSIZE)[:, None] == jnp.arange(groups_here)[None, :]
    row_prompt = jnp.sum(jnp.where(member, prompt_len[None, :], 0), axis=1)
    positions = (row_prompt + own_len).astype(jnp.float32)
    query = rotate(qkv[:, 0].reshape(local_rows, heads_here, HS), positions).astype(jnp.bfloat16)
    key_new = rotate(qkv[:, 1].reshape(local_rows, heads_here, HS), positions).astype(jnp.bfloat16)
    value_new = qkv[:, 2].reshape(local_rows, heads_here, HS).astype(jnp.bfloat16)
    scale = 1.0 / math.sqrt(HS)
    longest = prefix_keys.shape[1]
    own_count = own_keys.shape[1]
    grouped = query.reshape(groups_here, GSIZE, heads_here, HS)
    pre_keys = prefix_keys.reshape(groups_here, longest, heads_here, HS)
    pre_vals = prefix_values.reshape(groups_here, longest, heads_here, HS)
    mine_keys = own_keys.reshape(local_rows, own_count, heads_here, HS)
    mine_vals = own_values.reshape(local_rows, own_count, heads_here, HS)
    pre_scores = (
        jnp.einsum("gqhd,gjhd->gqhj", grouped, pre_keys, preferred_element_type=jnp.float32) * scale
    )
    pre_scores = jnp.where(
        jnp.arange(longest)[None, None, None, :] < prompt_len[:, None, None, None],
        pre_scores,
        -jnp.inf,
    )
    own_scores = (
        jnp.einsum("rhd,rthd->rht", query, mine_keys, preferred_element_type=jnp.float32) * scale
    )
    own_scores = jnp.where(
        jnp.arange(own_count)[None, None, :] < own_len[:, None, None], own_scores, -jnp.inf
    )
    self_scores = (
        jnp.einsum("rhd,rhd->rh", query, key_new, preferred_element_type=jnp.float32) * scale
    )
    pre_peak = jnp.max(pre_scores, axis=-1).reshape(local_rows, heads_here)
    peak = jnp.maximum(jnp.maximum(pre_peak, jnp.max(own_scores, axis=-1)), self_scores)
    pre_exp = jnp.exp(pre_scores - peak.reshape(groups_here, GSIZE, heads_here)[..., None])
    own_exp = jnp.exp(own_scores - peak[..., None])
    self_exp = jnp.exp(self_scores - peak)
    denom = (
        jnp.sum(pre_exp, axis=-1).reshape(local_rows, heads_here)
        + jnp.sum(own_exp, axis=-1)
        + self_exp
    )
    mixed = jnp.einsum(
        "gqhj,gjhd->gqhd",
        pre_exp.astype(jnp.bfloat16),
        pre_vals,
        preferred_element_type=jnp.float32,
    )
    mixed = mixed.reshape(local_rows, heads_here, HS)
    mixed = mixed + jnp.einsum(
        "rht,rthd->rhd", own_exp.astype(jnp.bfloat16), mine_vals, preferred_element_type=jnp.float32
    )
    mixed = mixed + self_exp.astype(jnp.bfloat16).astype(jnp.float32)[..., None] * value_new.astype(
        jnp.float32
    )
    attended = (mixed / denom[..., None]).astype(jnp.bfloat16)
    transposed = jnp.transpose(attended, (2, 1, 0))
    slices = lax.all_to_all(transposed, "grp", split_axis=0, concat_axis=2, tiled=True)
    dim_here = slices.shape[0]
    slices = jnp.moveaxis(head_gather(slices), 0, 1).reshape(dim_here, heads_here * head_count, -1)
    out_blocks = head_exchange(
        w_attn_out.reshape(dim_here, heads_here, head_count, width_here), 2
    )
    out_blocks = jnp.moveaxis(out_blocks, 0, 1).reshape(dim_here, heads_here * head_count, width_here)
    units = w_in.shape[1]
    down_blocks = head_exchange(w_down.reshape(units, head_count, width_here), 1).reshape(
        units * head_count, width_here
    )
    in_blocks = head_exchange(w_in.reshape(head_count, width_here, units), 0)
    in_blocks = jnp.moveaxis(in_blocks, 0, 1).reshape(width_here, head_count * units)
    partial = jnp.dot(gathered, in_blocks, preferred_element_type=jnp.float32)
    partial = head_exchange(partial.astype(jnp.bfloat16).reshape(-1, head_count, units), 1)
    hidden = jax.nn.gelu(
        jnp.sum(partial.astype(jnp.float32), axis=0) + b_in.astype(jnp.float32),
        approximate=True,
    ).astype(jnp.bfloat16)
    hidden = jnp.moveaxis(head_gather(hidden), 0, 1).reshape(hidden.shape[0], -1)
    mlp_part = jnp.dot(hidden, down_blocks, preferred_element_type=jnp.float32)
    attn_part = jnp.einsum("dkr,dkf->rf", slices, out_blocks, preferred_element_type=jnp.float32)
    combined = mlp_part + attn_part
    half_width = width_here // 2
    mine = lax.dynamic_slice_in_dim(combined, parity * half_width, half_width, axis=1)
    theirs = lax.dynamic_slice_in_dim(combined, (1 - parity) * half_width, half_width, axis=1)
    got = lax.ppermute(
        theirs.astype(jnp.bfloat16), "grp", [(i, i ^ 1) for i in range(grp_count)]
    )
    pair_sum = (mine + got.astype(jnp.float32)).astype(jnp.bfloat16)
    pieces = lax.all_to_all(
        pair_sum.reshape(grp_count, local_rows, half_width), "grp", 0, 0, tiled=True
    ).reshape(grp_count // 2, 2, local_rows, half_width)
    summed = jnp.sum(pieces.astype(jnp.float32), axis=0)
    summed = jnp.transpose(summed, (1, 0, 2)).reshape(local_rows, width_here)
    total = activations.astype(jnp.float32) + b_down.astype(jnp.float32)[None, :] + summed
    return total.astype(jnp.bfloat16)


def solution(mesh):
    in_specs = (
        P("grp", "head"),
        P(),
        P(),
        P("grp", None, "head"),
        P("grp", None, "head"),
        P("grp", None, "head"),
        P("grp", None, "head"),
        P("grp", None, "head"),
        P("grp"),
        P("grp"),
        P("grp", "head", None),
        P(None, ("grp", "head")),
        P(("grp", "head")),
        P(("grp", "head"), None),
        P("head"),
    )
    out_specs = P("grp", "head")
    return jax.shard_map(local, mesh=mesh, in_specs=in_specs, out_specs=out_specs, check_vma=False)
```

```python
import math

import jax
import jax.numpy as jnp
from jax import lax
from jax.sharding import PartitionSpec as P

HS = 256
ROT = 64
GSIZE = 16


def normalize(rows, gain, shift):
    floats = rows.astype(jnp.float32)
    center = floats - jnp.mean(floats, axis=-1, keepdims=True)
    spread = jnp.mean(center * center, axis=-1, keepdims=True)
    return (
        center * lax.rsqrt(spread + 1e-05) * gain.astype(jnp.float32) + shift.astype(jnp.float32)
    ).astype(jnp.bfloat16)


def rotate(values, positions):
    half = ROT // 2
    index = jnp.arange(half, dtype=jnp.float32)
    freqs = jnp.power(jnp.float32(10000.0), -2.0 * index / ROT)
    angle = positions[:, None, None] * freqs[None, None, :]
    cosine = jnp.cos(angle)
    sine = jnp.sin(angle)
    pairs = values[..., :ROT].reshape(values.shape[:-1] + (half, 2))
    first = pairs[..., 0]
    second = pairs[..., 1]
    turned = jnp.stack([first * cosine - second * sine, second * cosine + first * sine], axis=-1)
    turned = turned.reshape(values.shape[:-1] + (ROT,))
    return jnp.concatenate([turned, values[..., ROT:]], axis=-1)


def head_exchange(pieces, axis, ordered=True):
    count = lax.axis_size("head")
    here = lax.axis_index("head")
    received = []
    for shift in range(count):
        piece = lax.dynamic_index_in_dim(pieces, (here + shift) % count, axis, keepdims=False)
        if shift:
            piece = lax.ppermute(piece, "head", [(i, (i + shift) % count) for i in range(count)])
        received.append(piece)
    stacked = jnp.stack(received, axis=0)
    if not ordered:
        return stacked
    return jnp.take(stacked, (here - jnp.arange(count)) % count, axis=0)


def head_gather(piece, ordered=True):
    count = lax.axis_size("head")
    here = lax.axis_index("head")
    received = [piece]
    for shift in range(1, count):
        received.append(lax.ppermute(piece, "head", [(i, (i + shift) % count) for i in range(count)]))
    stacked = jnp.stack(received, axis=0)
    if not ordered:
        return stacked
    return jnp.take(stacked, (here - jnp.arange(count)) % count, axis=0)


def head_scatter_unordered(pieces, axis):
    count = lax.axis_size("head")
    received = []
    for shift in range(count):
        piece = lax.index_in_dim(pieces, (-shift) % count, axis, keepdims=False)
        if shift:
            piece = lax.ppermute(piece, "head", [(i, (i + shift) % count) for i in range(count)])
        received.append(piece)
    return jnp.stack(received, axis=0)


def local(
    activations,
    ln_gain,
    ln_bias,
    w_qkv,
    prefix_keys,
    prefix_values,
    own_keys,
    own_values,
    prompt_len,
    own_len,
    w_attn_out,
    w_in,
    b_in,
    w_down,
    b_down,
):
    grp_count = lax.axis_size("grp")
    head_count = lax.axis_size("head")
    width_here = activations.shape[1]
    full_rows = jnp.moveaxis(head_gather(activations), 0, 1).reshape(activations.shape[0], -1)
    normed = normalize(full_rows, ln_gain, ln_bias)
    local_rows = normed.shape[0]
    groups_here = prompt_len.shape[0]
    quarter = lax.dynamic_slice_in_dim(normed, lax.axis_index("head") * width_here, width_here, axis=1)
    block = w_qkv.shape[0]
    pair_rows = normed.reshape(local_rows, grp_count // 2, 2 * block)
    outgoing = jnp.concatenate(
        [
            jnp.repeat(pair_rows, 2, axis=1),
            jnp.broadcast_to(quarter[:, None, :], (local_rows, grp_count, width_here)),
        ],
        axis=2,
    )
    incoming = lax.all_to_all(outgoing, "grp", split_axis=1, concat_axis=0, tiled=True).reshape(
        grp_count * local_rows, 2 * block + width_here
    )
    columns = incoming[:, : 2 * block]
    gathered = incoming[:, 2 * block :]
    parity = lax.axis_index("grp") % 2
    half = w_qkv.shape[2] // 2
    own = lax.dynamic_slice_in_dim(w_qkv, parity * half, half, axis=2)
    other = lax.dynamic_slice_in_dim(w_qkv, (1 - parity) * half, half, axis=2)
    sibling = lax.ppermute(other, "grp", [(i, i ^ 1) for i in range(grp_count)])
    pair_weights = jnp.where(
        parity == 0,
        jnp.concatenate([own, sibling], axis=0),
        jnp.concatenate([sibling, own], axis=0),
    )
    term = jnp.einsum(
        "rf,fch->rch", columns, pair_weights, preferred_element_type=jnp.float32
    ).astype(jnp.bfloat16)
    received = lax.all_to_all(
        term.reshape(grp_count, local_rows, 3, half), "grp", 0, 0, tiled=True
    ).reshape(grp_count // 2, 2, local_rows, 3, half)
    qkv = jnp.sum(received.astype(jnp.float32), axis=0)
    qkv = jnp.transpose(qkv, (1, 2, 0, 3)).reshape(local_rows, 3, 2 * half)
    heads_here = w_qkv.shape[2] // HS
    member = (jnp.arange(local_rows) // GSIZE)[:, None] == jnp.arange(groups_here)[None, :]
    row_prompt = jnp.sum(jnp.where(member, prompt_len[None, :], 0), axis=1)
    positions = (row_prompt + own_len).astype(jnp.float32)
    query = rotate(qkv[:, 0].reshape(local_rows, heads_here, HS), positions).astype(jnp.bfloat16)
    key_new = rotate(qkv[:, 1].reshape(local_rows, heads_here, HS), positions).astype(jnp.bfloat16)
    value_new = qkv[:, 2].reshape(local_rows, heads_here, HS).astype(jnp.bfloat16)
    scale = 1.0 / math.sqrt(HS)
    longest = prefix_keys.shape[1]
    own_count = own_keys.shape[1]
    grouped = query.reshape(groups_here, GSIZE, heads_here, HS)
    pre_keys = prefix_keys.reshape(groups_here, longest, heads_here, HS)
    pre_vals = prefix_values.reshape(groups_here, longest, heads_here, HS)
    mine_keys = own_keys.reshape(local_rows, own_count, heads_here, HS)
    mine_vals = own_values.reshape(local_rows, own_count, heads_here, HS)
    pre_scores = (
        jnp.einsum("gqhd,gjhd->gqhj", grouped, pre_keys, preferred_element_type=jnp.float32) * scale
    )
    pre_scores = jnp.where(
        jnp.arange(longest)[None, None, None, :] < prompt_len[:, None, None, None],
        pre_scores,
        -jnp.inf,
    )
    own_scores = (
        jnp.einsum("rhd,rthd->rht", query, mine_keys, preferred_element_type=jnp.float32) * scale
    )
    own_scores = jnp.where(
        jnp.arange(own_count)[None, None, :] < own_len[:, None, None], own_scores, -jnp.inf
    )
    self_scores = (
        jnp.einsum("rhd,rhd->rh", query, key_new, preferred_element_type=jnp.float32) * scale
    )
    pre_peak = jnp.max(pre_scores, axis=-1).reshape(local_rows, heads_here)
    peak = jnp.maximum(jnp.maximum(pre_peak, jnp.max(own_scores, axis=-1)), self_scores)
    pre_exp = jnp.exp(pre_scores - peak.reshape(groups_here, GSIZE, heads_here)[..., None])
    own_exp = jnp.exp(own_scores - peak[..., None])
    self_exp = jnp.exp(self_scores - peak)
    denom = (
        jnp.sum(pre_exp, axis=-1).reshape(local_rows, heads_here)
        + jnp.sum(own_exp, axis=-1)
        + self_exp
    )
    mixed = jnp.einsum(
        "gqhj,gjhd->gqhd",
        pre_exp.astype(jnp.bfloat16),
        pre_vals,
        preferred_element_type=jnp.float32,
    )
    mixed = mixed.reshape(local_rows, heads_here, HS)
    mixed = mixed + jnp.einsum(
        "rht,rthd->rhd", own_exp.astype(jnp.bfloat16), mine_vals, preferred_element_type=jnp.float32
    )
    mixed = mixed + self_exp.astype(jnp.bfloat16).astype(jnp.float32)[..., None] * value_new.astype(
        jnp.float32
    )
    attended = (mixed / denom[..., None]).astype(jnp.bfloat16)
    transposed = jnp.transpose(attended, (2, 1, 0))
    slices = lax.all_to_all(transposed, "grp", split_axis=0, concat_axis=2, tiled=True)
    dim_here = slices.shape[0]
    slices = jnp.moveaxis(head_gather(slices, ordered=False), 0, 1).reshape(dim_here, heads_here * head_count, -1)
    out_blocks = head_exchange(
        w_attn_out.reshape(dim_here, heads_here, head_count, width_here), 2, ordered=False
    )
    out_blocks = jnp.moveaxis(out_blocks, 0, 1).reshape(dim_here, heads_here * head_count, width_here)
    units = w_in.shape[1]
    down_blocks = head_exchange(w_down.reshape(units, head_count, width_here), 1, ordered=False).reshape(
        units * head_count, width_here
    )
    in_blocks = head_exchange(w_in.reshape(head_count, width_here, units), 0, ordered=False)
    in_blocks = jnp.moveaxis(in_blocks, 0, 1).reshape(width_here, head_count * units)
    partial = jnp.dot(gathered, in_blocks, preferred_element_type=jnp.float32)
    partial = head_scatter_unordered(partial.astype(jnp.bfloat16).reshape(-1, head_count, units), 1)
    hidden = jax.nn.gelu(
        jnp.sum(partial.astype(jnp.float32), axis=0) + b_in.astype(jnp.float32),
        approximate=True,
    ).astype(jnp.bfloat16)
    hidden = jnp.moveaxis(head_gather(hidden, ordered=False), 0, 1).reshape(hidden.shape[0], -1)
    mlp_part = jnp.dot(hidden, down_blocks, preferred_element_type=jnp.float32)
    attn_part = jnp.einsum("dkr,dkf->rf", slices, out_blocks, preferred_element_type=jnp.float32)
    combined = mlp_part + attn_part
    half_width = width_here // 2
    mine = lax.dynamic_slice_in_dim(combined, parity * half_width, half_width, axis=1)
    theirs = lax.dynamic_slice_in_dim(combined, (1 - parity) * half_width, half_width, axis=1)
    got = lax.ppermute(
        theirs.astype(jnp.bfloat16), "grp", [(i, i ^ 1) for i in range(grp_count)]
    )
    pair_sum = (mine + got.astype(jnp.float32)).astype(jnp.bfloat16)
    pieces = lax.all_to_all(
        pair_sum.reshape(grp_count, local_rows, half_width), "grp", 0, 0, tiled=True
    ).reshape(grp_count // 2, 2, local_rows, half_width)
    summed = jnp.sum(pieces.astype(jnp.float32), axis=0)
    summed = jnp.transpose(summed, (1, 0, 2)).reshape(local_rows, width_here)
    total = activations.astype(jnp.float32) + b_down.astype(jnp.float32)[None, :] + summed
    return total.astype(jnp.bfloat16)


def solution(mesh):
    in_specs = (
        P("grp", "head"),
        P(),
        P(),
        P("grp", None, "head"),
        P("grp", None, "head"),
        P("grp", None, "head"),
        P("grp", None, "head"),
        P("grp", None, "head"),
        P("grp"),
        P("grp"),
        P("grp", "head", None),
        P(None, ("grp", "head")),
        P(("grp", "head")),
        P(("grp", "head"), None),
        P("head"),
    )
    out_specs = P("grp", "head")
    return jax.shard_map(local, mesh=mesh, in_specs=in_specs, out_specs=out_specs, check_vma=False)
```

```python
import math

import jax
import jax.numpy as jnp
from jax import lax
from jax.sharding import PartitionSpec as P

HS = 256
ROT = 64
GSIZE = 16


def normalize(rows, gain, shift):
    floats = rows.astype(jnp.float32)
    center = floats - jnp.mean(floats, axis=-1, keepdims=True)
    spread = jnp.mean(center * center, axis=-1, keepdims=True)
    return (
        center * lax.rsqrt(spread + 1e-05) * gain.astype(jnp.float32) + shift.astype(jnp.float32)
    ).astype(jnp.bfloat16)


def rotate(values, positions):
    half = ROT // 2
    index = jnp.arange(half, dtype=jnp.float32)
    freqs = jnp.power(jnp.float32(10000.0), -2.0 * index / ROT)
    angle = positions[:, None, None] * freqs[None, None, :]
    cosine = jnp.cos(angle)
    sine = jnp.sin(angle)
    pairs = values[..., :ROT].reshape(values.shape[:-1] + (half, 2))
    first = pairs[..., 0]
    second = pairs[..., 1]
    turned = jnp.stack([first * cosine - second * sine, second * cosine + first * sine], axis=-1)
    turned = turned.reshape(values.shape[:-1] + (ROT,))
    return jnp.concatenate([turned, values[..., ROT:]], axis=-1)


def head_exchange(pieces, axis, ordered=True):
    count = lax.axis_size("head")
    here = lax.axis_index("head")
    received = []
    for shift in range(count):
        piece = lax.dynamic_index_in_dim(pieces, (here + shift) % count, axis, keepdims=False)
        if shift:
            piece = lax.ppermute(piece, "head", [(i, (i + shift) % count) for i in range(count)])
        received.append(piece)
    stacked = jnp.stack(received, axis=0)
    if not ordered:
        return stacked
    return jnp.take(stacked, (here - jnp.arange(count)) % count, axis=0)


def head_gather(piece, ordered=True):
    count = lax.axis_size("head")
    here = lax.axis_index("head")
    received = [piece]
    for shift in range(1, count):
        received.append(lax.ppermute(piece, "head", [(i, (i + shift) % count) for i in range(count)]))
    stacked = jnp.stack(received, axis=0)
    if not ordered:
        return stacked
    return jnp.take(stacked, (here - jnp.arange(count)) % count, axis=0)


def local(
    activations,
    ln_gain,
    ln_bias,
    w_qkv,
    prefix_keys,
    prefix_values,
    own_keys,
    own_values,
    prompt_len,
    own_len,
    w_attn_out,
    w_in,
    b_in,
    w_down,
    b_down,
):
    grp_count = lax.axis_size("grp")
    head_count = lax.axis_size("head")
    width_here = activations.shape[1]
    full_rows = jnp.moveaxis(head_gather(activations), 0, 1).reshape(activations.shape[0], -1)
    normed = normalize(full_rows, ln_gain, ln_bias)
    local_rows = normed.shape[0]
    groups_here = prompt_len.shape[0]
    gathered = lax.all_gather(normed, "grp", axis=0, tiled=True)
    block = w_qkv.shape[0]
    pair_rows = normed.reshape(local_rows, grp_count // 2, 2 * block)
    columns = lax.all_to_all(
        jnp.repeat(pair_rows, 2, axis=1), "grp", split_axis=1, concat_axis=0, tiled=True
    ).reshape(grp_count * local_rows, 2 * block)
    parity = lax.axis_index("grp") % 2
    half = w_qkv.shape[2] // 2
    own = lax.dynamic_slice_in_dim(w_qkv, parity * half, half, axis=2)
    other = lax.dynamic_slice_in_dim(w_qkv, (1 - parity) * half, half, axis=2)
    sibling = lax.ppermute(other, "grp", [(i, i ^ 1) for i in range(grp_count)])
    pair_weights = jnp.where(
        parity == 0,
        jnp.concatenate([own, sibling], axis=0),
        jnp.concatenate([sibling, own], axis=0),
    )
    term = jnp.einsum(
        "rf,fch->rch", columns, pair_weights, preferred_element_type=jnp.float32
    ).astype(jnp.bfloat16)
    received = lax.all_to_all(
        term.reshape(grp_count, local_rows, 3, half), "grp", 0, 0, tiled=True
    ).reshape(grp_count // 2, 2, local_rows, 3, half)
    qkv = jnp.sum(received.astype(jnp.float32), axis=0)
    qkv = jnp.transpose(qkv, (1, 2, 0, 3)).reshape(local_rows, 3, 2 * half)
    heads_here = w_qkv.shape[2] // HS
    member = (jnp.arange(local_rows) // GSIZE)[:, None] == jnp.arange(groups_here)[None, :]
    row_prompt = jnp.sum(jnp.where(member, prompt_len[None, :], 0), axis=1)
    positions = (row_prompt + own_len).astype(jnp.float32)
    query = rotate(qkv[:, 0].reshape(local_rows, heads_here, HS), positions).astype(jnp.bfloat16)
    key_new = rotate(qkv[:, 1].reshape(local_rows, heads_here, HS), positions).astype(jnp.bfloat16)
    value_new = qkv[:, 2].reshape(local_rows, heads_here, HS).astype(jnp.bfloat16)
    scale = 1.0 / math.sqrt(HS)
    longest = prefix_keys.shape[1]
    own_count = own_keys.shape[1]
    grouped = query.reshape(groups_here, GSIZE, heads_here, HS)
    pre_keys = prefix_keys.reshape(groups_here, longest, heads_here, HS)
    pre_vals = prefix_values.reshape(groups_here, longest, heads_here, HS)
    mine_keys = own_keys.reshape(local_rows, own_count, heads_here, HS)
    mine_vals = own_values.reshape(local_rows, own_count, heads_here, HS)
    pre_scores = (
        jnp.einsum("gqhd,gjhd->gqhj", grouped, pre_keys, preferred_element_type=jnp.float32) * scale
    )
    pre_scores = jnp.where(
        jnp.arange(longest)[None, None, None, :] < prompt_len[:, None, None, None],
        pre_scores,
        -jnp.inf,
    )
    own_scores = (
        jnp.einsum("rhd,rthd->rht", query, mine_keys, preferred_element_type=jnp.float32) * scale
    )
    own_scores = jnp.where(
        jnp.arange(own_count)[None, None, :] < own_len[:, None, None], own_scores, -jnp.inf
    )
    self_scores = (
        jnp.einsum("rhd,rhd->rh", query, key_new, preferred_element_type=jnp.float32) * scale
    )
    pre_peak = jnp.max(pre_scores, axis=-1).reshape(local_rows, heads_here)
    peak = jnp.maximum(jnp.maximum(pre_peak, jnp.max(own_scores, axis=-1)), self_scores)
    pre_exp = jnp.exp(pre_scores - peak.reshape(groups_here, GSIZE, heads_here)[..., None])
    own_exp = jnp.exp(own_scores - peak[..., None])
    self_exp = jnp.exp(self_scores - peak)
    denom = (
        jnp.sum(pre_exp, axis=-1).reshape(local_rows, heads_here)
        + jnp.sum(own_exp, axis=-1)
        + self_exp
    )
    mixed = jnp.einsum(
        "gqhj,gjhd->gqhd",
        pre_exp.astype(jnp.bfloat16),
        pre_vals,
        preferred_element_type=jnp.float32,
    )
    mixed = mixed.reshape(local_rows, heads_here, HS)
    mixed = mixed + jnp.einsum(
        "rht,rthd->rhd", own_exp.astype(jnp.bfloat16), mine_vals, preferred_element_type=jnp.float32
    )
    mixed = mixed + self_exp.astype(jnp.bfloat16).astype(jnp.float32)[..., None] * value_new.astype(
        jnp.float32
    )
    attended = (mixed / denom[..., None]).astype(jnp.bfloat16)
    transposed = jnp.transpose(attended, (2, 1, 0))
    slices = lax.all_to_all(transposed, "grp", split_axis=0, concat_axis=2, tiled=True)
    dim_here = slices.shape[0]
    slices = jnp.moveaxis(head_gather(slices, ordered=False), 0, 1).reshape(dim_here, heads_here * head_count, -1)
    out_blocks = head_exchange(
        w_attn_out.reshape(dim_here, heads_here, head_count, width_here), 2, ordered=False
    )
    out_blocks = jnp.moveaxis(out_blocks, 0, 1).reshape(dim_here, heads_here * head_count, width_here)
    units = w_in.shape[1]
    down_blocks = head_exchange(w_down.reshape(units, head_count, width_here), 1, ordered=False).reshape(
        units * head_count, width_here
    )
    hidden = jax.nn.gelu(
        jnp.dot(
            gathered,
            w_in,
            preferred_element_type=jnp.float32,
        )
        + b_in.astype(jnp.float32),
        approximate=True,
    ).astype(jnp.bfloat16)
    hidden = jnp.moveaxis(head_gather(hidden, ordered=False), 0, 1).reshape(hidden.shape[0], -1)
    mlp_part = jnp.dot(hidden, down_blocks, preferred_element_type=jnp.float32)
    attn_part = jnp.einsum("dkr,dkf->rf", slices, out_blocks, preferred_element_type=jnp.float32)
    combined = mlp_part + attn_part
    half_width = width_here // 2
    mine = lax.dynamic_slice_in_dim(combined, parity * half_width, half_width, axis=1)
    theirs = lax.dynamic_slice_in_dim(combined, (1 - parity) * half_width, half_width, axis=1)
    got = lax.ppermute(
        theirs.astype(jnp.bfloat16), "grp", [(i, i ^ 1) for i in range(grp_count)]
    )
    pair_sum = (mine + got.astype(jnp.float32)).astype(jnp.bfloat16)
    pieces = lax.all_to_all(
        pair_sum.reshape(grp_count, local_rows, half_width), "grp", 0, 0, tiled=True
    ).reshape(grp_count // 2, 2, local_rows, half_width)
    summed = jnp.sum(pieces.astype(jnp.float32), axis=0)
    summed = jnp.transpose(summed, (1, 0, 2)).reshape(local_rows, width_here)
    total = activations.astype(jnp.float32) + b_down.astype(jnp.float32)[None, :] + summed
    return total.astype(jnp.bfloat16)


def solution(mesh):
    in_specs = (
        P("grp", "head"),
        P(),
        P(),
        P("grp", None, "head"),
        P("grp", None, "head"),
        P("grp", None, "head"),
        P("grp", None, "head"),
        P("grp", None, "head"),
        P("grp"),
        P("grp"),
        P("grp", "head", None),
        P(None, ("grp", "head")),
        P(("grp", "head")),
        P(("grp", "head"), None),
        P("head"),
    )
    out_specs = P("grp", "head")
    return jax.shard_map(local, mesh=mesh, in_specs=in_specs, out_specs=out_specs, check_vma=False)
```

```python
import math

import jax
import jax.numpy as jnp
from jax import lax
from jax.sharding import PartitionSpec as P

HS = 256
ROT = 64
GSIZE = 16


def normalize(rows, gain, shift):
    floats = rows.astype(jnp.float32)
    center = floats - jnp.mean(floats, axis=-1, keepdims=True)
    spread = jnp.mean(center * center, axis=-1, keepdims=True)
    return (
        center * lax.rsqrt(spread + 1e-05) * gain.astype(jnp.float32) + shift.astype(jnp.float32)
    ).astype(jnp.bfloat16)


def rotate(values, positions):
    half = ROT // 2
    index = jnp.arange(half, dtype=jnp.float32)
    freqs = jnp.power(jnp.float32(10000.0), -2.0 * index / ROT)
    angle = positions[:, None, None] * freqs[None, None, :]
    cosine = jnp.cos(angle)
    sine = jnp.sin(angle)
    pairs = values[..., :ROT].reshape(values.shape[:-1] + (half, 2))
    first = pairs[..., 0]
    second = pairs[..., 1]
    turned = jnp.stack([first * cosine - second * sine, second * cosine + first * sine], axis=-1)
    turned = turned.reshape(values.shape[:-1] + (ROT,))
    return jnp.concatenate([turned, values[..., ROT:]], axis=-1)


def head_exchange(pieces, axis):
    count = lax.axis_size("head")
    here = lax.axis_index("head")
    received = []
    for shift in range(count):
        piece = lax.dynamic_index_in_dim(pieces, (here + shift) % count, axis, keepdims=False)
        if shift:
            piece = lax.ppermute(piece, "head", [(i, (i + shift) % count) for i in range(count)])
        received.append(piece)
    stacked = jnp.stack(received, axis=0)
    return jnp.take(stacked, (here - jnp.arange(count)) % count, axis=0)


def head_gather(piece):
    count = lax.axis_size("head")
    here = lax.axis_index("head")
    received = [piece]
    for shift in range(1, count):
        received.append(lax.ppermute(piece, "head", [(i, (i + shift) % count) for i in range(count)]))
    stacked = jnp.stack(received, axis=0)
    return jnp.take(stacked, (here - jnp.arange(count)) % count, axis=0)


def local(
    activations,
    ln_gain,
    ln_bias,
    w_qkv,
    prefix_keys,
    prefix_values,
    own_keys,
    own_values,
    prompt_len,
    own_len,
    w_attn_out,
    w_in,
    b_in,
    w_down,
    b_down,
):
    grp_count = lax.axis_size("grp")
    head_count = lax.axis_size("head")
    width_here = activations.shape[1]
    full_rows = jnp.moveaxis(head_gather(activations), 0, 1).reshape(activations.shape[0], -1)
    normed = normalize(full_rows, ln_gain, ln_bias)
    local_rows = normed.shape[0]
    groups_here = prompt_len.shape[0]
    gathered = lax.all_gather(normed, "grp", axis=0, tiled=True)
    block = w_qkv.shape[0]
    pair_rows = normed.reshape(local_rows, grp_count // 2, 2 * block)
    columns = lax.all_to_all(
        jnp.repeat(pair_rows, 2, axis=1), "grp", split_axis=1, concat_axis=0, tiled=True
    ).reshape(grp_count * local_rows, 2 * block)
    parity = lax.axis_index("grp") % 2
    half = w_qkv.shape[2] // 2
    own = lax.dynamic_slice_in_dim(w_qkv, parity * half, half, axis=2)
    other = lax.dynamic_slice_in_dim(w_qkv, (1 - parity) * half, half, axis=2)
    sibling = lax.ppermute(other, "grp", [(i, i ^ 1) for i in range(grp_count)])
    pair_weights = jnp.where(
        parity == 0,
        jnp.concatenate([own, sibling], axis=0),
        jnp.concatenate([sibling, own], axis=0),
    )
    term = jnp.einsum(
        "rf,fch->rch", columns, pair_weights, preferred_element_type=jnp.float32
    ).astype(jnp.bfloat16)
    def exchange(part):
        which = part.shape[1]
        got = lax.all_to_all(
            part.reshape(grp_count, local_rows, which, half), "grp", 0, 0, tiled=True
        ).reshape(grp_count // 2, 2, local_rows, which, half)
        got = jnp.sum(got.astype(jnp.float32), axis=0)
        return jnp.transpose(got, (1, 2, 0, 3)).reshape(local_rows, which, 2 * half)

    q_sum = exchange(term[:, :1])
    kv_sum = exchange(term[:, 1:])
    heads_here = w_qkv.shape[2] // HS
    member = (jnp.arange(local_rows) // GSIZE)[:, None] == jnp.arange(groups_here)[None, :]
    row_prompt = jnp.sum(jnp.where(member, prompt_len[None, :], 0), axis=1)
    positions = (row_prompt + own_len).astype(jnp.float32)
    query = rotate(q_sum[:, 0].reshape(local_rows, heads_here, HS), positions).astype(jnp.bfloat16)
    key_new = rotate(kv_sum[:, 0].reshape(local_rows, heads_here, HS), positions).astype(jnp.bfloat16)
    value_new = kv_sum[:, 1].reshape(local_rows, heads_here, HS).astype(jnp.bfloat16)
    scale = 1.0 / math.sqrt(HS)
    longest = prefix_keys.shape[1]
    own_count = own_keys.shape[1]
    grouped = query.reshape(groups_here, GSIZE, heads_here, HS)
    pre_keys = prefix_keys.reshape(groups_here, longest, heads_here, HS)
    pre_vals = prefix_values.reshape(groups_here, longest, heads_here, HS)
    mine_keys = own_keys.reshape(local_rows, own_count, heads_here, HS)
    mine_vals = own_values.reshape(local_rows, own_count, heads_here, HS)
    pre_scores = (
        jnp.einsum("gqhd,gjhd->gqhj", grouped, pre_keys, preferred_element_type=jnp.float32) * scale
    )
    pre_scores = jnp.where(
        jnp.arange(longest)[None, None, None, :] < prompt_len[:, None, None, None],
        pre_scores,
        -jnp.inf,
    )
    own_scores = (
        jnp.einsum("rhd,rthd->rht", query, mine_keys, preferred_element_type=jnp.float32) * scale
    )
    own_scores = jnp.where(
        jnp.arange(own_count)[None, None, :] < own_len[:, None, None], own_scores, -jnp.inf
    )
    self_scores = (
        jnp.einsum("rhd,rhd->rh", query, key_new, preferred_element_type=jnp.float32) * scale
    )
    pre_peak = jnp.max(pre_scores, axis=-1).reshape(local_rows, heads_here)
    peak = jnp.maximum(jnp.maximum(pre_peak, jnp.max(own_scores, axis=-1)), self_scores)
    pre_exp = jnp.exp(pre_scores - peak.reshape(groups_here, GSIZE, heads_here)[..., None])
    own_exp = jnp.exp(own_scores - peak[..., None])
    self_exp = jnp.exp(self_scores - peak)
    denom = (
        jnp.sum(pre_exp, axis=-1).reshape(local_rows, heads_here)
        + jnp.sum(own_exp, axis=-1)
        + self_exp
    )
    mixed = jnp.einsum(
        "gqhj,gjhd->gqhd",
        pre_exp.astype(jnp.bfloat16),
        pre_vals,
        preferred_element_type=jnp.float32,
    )
    mixed = mixed.reshape(local_rows, heads_here, HS)
    mixed = mixed + jnp.einsum(
        "rht,rthd->rhd", own_exp.astype(jnp.bfloat16), mine_vals, preferred_element_type=jnp.float32
    )
    mixed = mixed + self_exp.astype(jnp.bfloat16).astype(jnp.float32)[..., None] * value_new.astype(
        jnp.float32
    )
    attended = (mixed / denom[..., None]).astype(jnp.bfloat16)
    transposed = jnp.transpose(attended, (2, 1, 0))
    slices = lax.all_to_all(transposed, "grp", split_axis=0, concat_axis=2, tiled=True)
    dim_here = slices.shape[0]
    slices = jnp.moveaxis(head_gather(slices), 0, 1).reshape(dim_here, heads_here * head_count, -1)
    out_blocks = head_exchange(
        w_attn_out.reshape(dim_here, heads_here, head_count, width_here), 2
    )
    out_blocks = jnp.moveaxis(out_blocks, 0, 1).reshape(dim_here, heads_here * head_count, width_here)
    units = w_in.shape[1]
    down_blocks = head_exchange(w_down.reshape(units, head_count, width_here), 1).reshape(
        units * head_count, width_here
    )
    hidden = jax.nn.gelu(
        jnp.dot(
            gathered,
            w_in,
            preferred_element_type=jnp.float32,
        )
        + b_in.astype(jnp.float32),
        approximate=True,
    ).astype(jnp.bfloat16)
    hidden = lax.all_gather(hidden, "head", axis=1, tiled=True)
    mlp_part = jnp.dot(hidden, down_blocks, preferred_element_type=jnp.float32)
    attn_part = jnp.einsum("dkr,dkf->rf", slices, out_blocks, preferred_element_type=jnp.float32)
    combined = mlp_part + attn_part
    half_width = width_here // 2
    mine = lax.dynamic_slice_in_dim(combined, parity * half_width, half_width, axis=1)
    theirs = lax.dynamic_slice_in_dim(combined, (1 - parity) * half_width, half_width, axis=1)
    got = lax.ppermute(
        theirs.astype(jnp.bfloat16), "grp", [(i, i ^ 1) for i in range(grp_count)]
    )
    pair_sum = (mine + got.astype(jnp.float32)).astype(jnp.bfloat16)
    pieces = lax.all_to_all(
        pair_sum.reshape(grp_count, local_rows, half_width), "grp", 0, 0, tiled=True
    ).reshape(grp_count // 2, 2, local_rows, half_width)
    summed = jnp.sum(pieces.astype(jnp.float32), axis=0)
    summed = jnp.transpose(summed, (1, 0, 2)).reshape(local_rows, width_here)
    total = activations.astype(jnp.float32) + b_down.astype(jnp.float32)[None, :] + summed
    return total.astype(jnp.bfloat16)


def solution(mesh):
    in_specs = (
        P("grp", "head"),
        P(),
        P(),
        P("grp", None, "head"),
        P("grp", None, "head"),
        P("grp", None, "head"),
        P("grp", None, "head"),
        P("grp", None, "head"),
        P("grp"),
        P("grp"),
        P("grp", "head", None),
        P(None, ("grp", "head")),
        P(("grp", "head")),
        P(("grp", "head"), None),
        P("head"),
    )
    out_specs = P("grp", "head")
    return jax.shard_map(local, mesh=mesh, in_specs=in_specs, out_specs=out_specs, check_vma=False)
```

```python
import math

import jax
import jax.numpy as jnp
from jax import lax
from jax.sharding import PartitionSpec as P

HS = 256
ROT = 64
GSIZE = 16


def normalize(rows, gain, shift):
    floats = rows.astype(jnp.float32)
    center = floats - jnp.mean(floats, axis=-1, keepdims=True)
    spread = jnp.mean(center * center, axis=-1, keepdims=True)
    return (
        center * lax.rsqrt(spread + 1e-05) * gain.astype(jnp.float32) + shift.astype(jnp.float32)
    ).astype(jnp.bfloat16)


def rotate(values, positions):
    half = ROT // 2
    index = jnp.arange(half, dtype=jnp.float32)
    freqs = jnp.power(jnp.float32(10000.0), -2.0 * index / ROT)
    angle = positions[:, None, None] * freqs[None, None, :]
    cosine = jnp.cos(angle)
    sine = jnp.sin(angle)
    pairs = values[..., :ROT].reshape(values.shape[:-1] + (half, 2))
    first = pairs[..., 0]
    second = pairs[..., 1]
    turned = jnp.stack([first * cosine - second * sine, second * cosine + first * sine], axis=-1)
    turned = turned.reshape(values.shape[:-1] + (ROT,))
    return jnp.concatenate([turned, values[..., ROT:]], axis=-1)


def head_exchange(pieces, axis):
    count = lax.axis_size("head")
    here = lax.axis_index("head")
    received = []
    for shift in range(count):
        piece = lax.dynamic_index_in_dim(pieces, (here + shift) % count, axis, keepdims=False)
        if shift:
            piece = lax.ppermute(piece, "head", [(i, (i + shift) % count) for i in range(count)])
        received.append(piece)
    stacked = jnp.stack(received, axis=0)
    return jnp.take(stacked, (here - jnp.arange(count)) % count, axis=0)


def head_gather(piece):
    count = lax.axis_size("head")
    here = lax.axis_index("head")
    received = [piece]
    for shift in range(1, count):
        received.append(lax.ppermute(piece, "head", [(i, (i + shift) % count) for i in range(count)]))
    stacked = jnp.stack(received, axis=0)
    return jnp.take(stacked, (here - jnp.arange(count)) % count, axis=0)


def local(
    activations,
    ln_gain,
    ln_bias,
    w_qkv,
    prefix_keys,
    prefix_values,
    own_keys,
    own_values,
    prompt_len,
    own_len,
    w_attn_out,
    w_in,
    b_in,
    w_down,
    b_down,
):
    grp_count = lax.axis_size("grp")
    head_count = lax.axis_size("head")
    width_here = activations.shape[1]
    full_rows = jnp.moveaxis(head_gather(activations), 0, 1).reshape(activations.shape[0], -1)
    normed = normalize(full_rows, ln_gain, ln_bias)
    local_rows = normed.shape[0]
    groups_here = prompt_len.shape[0]
    gathered = lax.all_gather(normed, "grp", axis=0, tiled=True)
    block = w_qkv.shape[0]
    pair_rows = normed.reshape(local_rows, grp_count // 2, 2 * block)
    columns = lax.all_to_all(
        jnp.repeat(pair_rows, 2, axis=1), "grp", split_axis=1, concat_axis=0, tiled=True
    ).reshape(grp_count * local_rows, 2 * block)
    parity = lax.axis_index("grp") % 2
    half = w_qkv.shape[2] // 2
    own = lax.dynamic_slice_in_dim(w_qkv, parity * half, half, axis=2)
    other = lax.dynamic_slice_in_dim(w_qkv, (1 - parity) * half, half, axis=2)
    sibling = lax.ppermute(other, "grp", [(i, i ^ 1) for i in range(grp_count)])
    pair_weights = jnp.where(
        parity == 0,
        jnp.concatenate([own, sibling], axis=0),
        jnp.concatenate([sibling, own], axis=0),
    )
    term = jnp.einsum(
        "rf,fch->rch", columns, pair_weights, preferred_element_type=jnp.float32
    ).astype(jnp.bfloat16)
    received = lax.all_to_all(
        term.reshape(grp_count, local_rows, 3, half), "grp", 0, 0, tiled=True
    ).reshape(grp_count // 2, 2, local_rows, 3, half)
    qkv = jnp.sum(received.astype(jnp.float32), axis=0)
    qkv = jnp.transpose(qkv, (1, 2, 0, 3)).reshape(local_rows, 3, 2 * half)
    heads_here = w_qkv.shape[2] // HS
    member = (jnp.arange(local_rows) // GSIZE)[:, None] == jnp.arange(groups_here)[None, :]
    row_prompt = jnp.sum(jnp.where(member, prompt_len[None, :], 0), axis=1)
    positions = (row_prompt + own_len).astype(jnp.float32)
    query = rotate(qkv[:, 0].reshape(local_rows, heads_here, HS), positions).astype(jnp.bfloat16)
    key_new = rotate(qkv[:, 1].reshape(local_rows, heads_here, HS), positions).astype(jnp.bfloat16)
    value_new = qkv[:, 2].reshape(local_rows, heads_here, HS).astype(jnp.bfloat16)
    scale = 1.0 / math.sqrt(HS)
    longest = prefix_keys.shape[1]
    own_count = own_keys.shape[1]
    grouped = query.reshape(groups_here, GSIZE, heads_here, HS)
    pre_keys = prefix_keys.reshape(groups_here, longest, heads_here, HS)
    pre_vals = prefix_values.reshape(groups_here, longest, heads_here, HS)
    mine_keys = own_keys.reshape(local_rows, own_count, heads_here, HS)
    mine_vals = own_values.reshape(local_rows, own_count, heads_here, HS)
    pre_scores = (
        jnp.einsum("gqhd,gjhd->gqhj", grouped, pre_keys, preferred_element_type=jnp.float32) * scale
    )
    pre_scores = jnp.where(
        jnp.arange(longest)[None, None, None, :] < prompt_len[:, None, None, None],
        pre_scores,
        -jnp.inf,
    )
    own_scores = (
        jnp.einsum("rhd,rthd->rht", query, mine_keys, preferred_element_type=jnp.float32) * scale
    )
    own_scores = jnp.where(
        jnp.arange(own_count)[None, None, :] < own_len[:, None, None], own_scores, -jnp.inf
    )
    self_scores = (
        jnp.einsum("rhd,rhd->rh", query, key_new, preferred_element_type=jnp.float32) * scale
    )
    pre_peak = jnp.max(pre_scores, axis=-1).reshape(local_rows, heads_here)
    peak = jnp.maximum(jnp.maximum(pre_peak, jnp.max(own_scores, axis=-1)), self_scores)
    pre_exp = jnp.exp(pre_scores - peak.reshape(groups_here, GSIZE, heads_here)[..., None])
    own_exp = jnp.exp(own_scores - peak[..., None])
    self_exp = jnp.exp(self_scores - peak)
    denom = (
        jnp.sum(pre_exp, axis=-1).reshape(local_rows, heads_here)
        + jnp.sum(own_exp, axis=-1)
        + self_exp
    )
    mixed = jnp.einsum(
        "gqhj,gjhd->gqhd",
        pre_exp.astype(jnp.bfloat16),
        pre_vals,
        preferred_element_type=jnp.float32,
    )
    mixed = mixed.reshape(local_rows, heads_here, HS)
    mixed = mixed + jnp.einsum(
        "rht,rthd->rhd", own_exp.astype(jnp.bfloat16), mine_vals, preferred_element_type=jnp.float32
    )
    mixed = mixed + self_exp.astype(jnp.bfloat16).astype(jnp.float32)[..., None] * value_new.astype(
        jnp.float32
    )
    attended = (mixed / denom[..., None]).astype(jnp.bfloat16)
    dim_here = HS // grp_count
    outgoing = jnp.broadcast_to(
        jnp.transpose(attended.reshape(local_rows, heads_here, grp_count, dim_here), (2, 0, 1, 3))[
            :, None
        ],
        (grp_count, head_count, local_rows, heads_here, dim_here),
    ).reshape(grp_count * head_count, local_rows, heads_here, dim_here)
    incoming = lax.all_to_all(outgoing, ("grp", "head"), 0, 0, tiled=True).reshape(
        grp_count, head_count, local_rows, heads_here, dim_here
    )
    slices = jnp.transpose(incoming, (4, 1, 3, 0, 2)).reshape(
        dim_here, head_count * heads_here, grp_count * local_rows
    )
    out_blocks = head_exchange(
        w_attn_out.reshape(dim_here, heads_here, head_count, width_here), 2
    )
    out_blocks = jnp.moveaxis(out_blocks, 0, 1).reshape(dim_here, heads_here * head_count, width_here)
    units = w_in.shape[1]
    down_blocks = head_exchange(w_down.reshape(units, head_count, width_here), 1).reshape(
        units * head_count, width_here
    )
    hidden = jax.nn.gelu(
        jnp.dot(
            gathered,
            w_in,
            preferred_element_type=jnp.float32,
        )
        + b_in.astype(jnp.float32),
        approximate=True,
    ).astype(jnp.bfloat16)
    hidden = lax.all_gather(hidden, "head", axis=1, tiled=True)
    mlp_part = jnp.dot(hidden, down_blocks, preferred_element_type=jnp.float32)
    attn_part = jnp.einsum("dkr,dkf->rf", slices, out_blocks, preferred_element_type=jnp.float32)
    combined = mlp_part + attn_part
    half_width = width_here // 2
    mine = lax.dynamic_slice_in_dim(combined, parity * half_width, half_width, axis=1)
    theirs = lax.dynamic_slice_in_dim(combined, (1 - parity) * half_width, half_width, axis=1)
    got = lax.ppermute(
        theirs.astype(jnp.bfloat16), "grp", [(i, i ^ 1) for i in range(grp_count)]
    )
    pair_sum = (mine + got.astype(jnp.float32)).astype(jnp.bfloat16)
    pieces = lax.all_to_all(
        pair_sum.reshape(grp_count, local_rows, half_width), "grp", 0, 0, tiled=True
    ).reshape(grp_count // 2, 2, local_rows, half_width)
    summed = jnp.sum(pieces.astype(jnp.float32), axis=0)
    summed = jnp.transpose(summed, (1, 0, 2)).reshape(local_rows, width_here)
    total = activations.astype(jnp.float32) + b_down.astype(jnp.float32)[None, :] + summed
    return total.astype(jnp.bfloat16)


def solution(mesh):
    in_specs = (
        P("grp", "head"),
        P(),
        P(),
        P("grp", None, "head"),
        P("grp", None, "head"),
        P("grp", None, "head"),
        P("grp", None, "head"),
        P("grp", None, "head"),
        P("grp"),
        P("grp"),
        P("grp", "head", None),
        P(None, ("grp", "head")),
        P(("grp", "head")),
        P(("grp", "head"), None),
        P("head"),
    )
    out_specs = P("grp", "head")
    return jax.shard_map(local, mesh=mesh, in_specs=in_specs, out_specs=out_specs, check_vma=False)
```
